1024 devices in a mesh: section: 2 (over core), ctx: 64 (over x, y), head: 8 (over z).
Axes of the slice: x: 8, y: 8, z: 8, core: 2. Of those that a mesh axis runs over, the one named last changes fastest.
Arguments:
- layer_in: bfloat16 [2, 8192, 8192], P('section', 'ctx', 'head'), may hold values from -200 to 200
- kv_in: bfloat16 [2, 8192, 2048], P('section', 'ctx', 'head'), may hold values from -12 to 12
- out_grad: bfloat16 [8192, 8192], P('ctx', 'head'), may hold values from -6 to 6
- sentences: int32 [8192], P('ctx'), may hold values from 0 to 255, never falling along the last dimension, each value on 1 to 96 neighbouring positions
- anchor_blocks: int32 [4], replicated, may hold values from 0 to 63, as said below
- anchor_pick: int32 [64, 2], P('ctx'), may hold values from 0 to 3, all different within a row
Outputs:
- input_grad: bfloat16 [2, 8192, 8192], P('section', 'ctx', 'head')
- kv_grad: bfloat16 [2, 8192, 2048], P('section', 'ctx', 'head')
The draws below stay inside these ranges and needn't reach their ends.
Inputs may be any that keep to these rules, and one draw needn't show every extreme that they name: `anchor_blocks`: the anchor blocks are distinct; anchor a lies among the tokens of a ctx index in the a-th of 4 equal ranges of ctx indices, so no two lie among the 128 tokens of one index of ctx.
All inputs are finite; a program needn't handle non-finite values.
Results may differ from the reference program's by a relative error of at most 0.0061.
Values may be sent and summed in bfloat16 or wider, within the bound.
No kernel may reach another device: no remote copies, remote signals or barrier semaphores. Data moves between devices by JAX's collectives and lax.ppermute only.
A program may use at most 32 MiB of HBM per device.

```python
import math
import jax
import jax.numpy as jnp
import numpy as np
from jax import lax

QUERY_HEADS = 64
KEY_VALUE_HEADS = 8
HEAD_SIZE = 128
ROWS_DEV = 128
BLK = 128
NANCH = 4
APICK = 2
DOCUMENT_TOKENS = 8192
NBLK = 64
N_CTX = 64


def common_key_rows(key):
    base_offset = jnp.clip(jax.random.normal(jax.random.fold_in(key, 7), (2, DOCUMENT_TOKENS, KEY_VALUE_HEADS, 2, HEAD_SIZE), jnp.float32), -6.0, 6.0)
    return base_offset


def draw_kv_in(key, part):
    return common_key_rows(key).reshape(2, DOCUMENT_TOKENS, 2 * KEY_VALUE_HEADS * HEAD_SIZE).astype(jnp.bfloat16)


def draw_layer_in(key, part):
    group_size = QUERY_HEADS // KEY_VALUE_HEADS
    query_rows = jnp.clip(jax.random.normal(jax.random.fold_in(key, 11), (2, DOCUMENT_TOKENS, KEY_VALUE_HEADS, group_size, HEAD_SIZE), jnp.float32), -6.0, 6.0)
    return query_rows.reshape(2, DOCUMENT_TOKENS, QUERY_HEADS * HEAD_SIZE).astype(jnp.bfloat16)


def draw_anchor_blocks(key, part):
    per_dev = ROWS_DEV // BLK
    span = N_CTX // NANCH
    owners = jnp.arange(NANCH, dtype=jnp.int32) * span + jax.random.randint(jax.random.fold_in(key, 1), (NANCH,), 0, span)
    local = jax.random.randint(jax.random.fold_in(key, 2), (NANCH,), 0, per_dev)
    return (owners * per_dev + local).astype(jnp.int32)


def levels(own_key, extent, cuts, least, largest):
    loudness = 1.0
    for axis_at, parts in cuts:
        steps = jax.random.uniform(jax.random.fold_in(jax.random.fold_in(own_key, 6), axis_at), (parts,), jnp.float32, least / len(cuts), largest / len(cuts))
        loudness = loudness * jnp.repeat(jnp.exp(steps), extent[axis_at] // parts).reshape((-1,) + (1,) * (len(extent) - 1 - axis_at))
    return loudness


def choose_distinct(own_key, rows, count, top, lift):
    order = jax.random.permutation(jax.random.fold_in(own_key, 1), count)
    pull = order
    for power in range(3):
        pull = pull * pull // count
    pull = pull * lift // count
    lots = jax.random.randint(jax.random.fold_in(own_key, 2), (rows, count), 0, 4096) + pull
    fixed_rows = jax.random.permutation(jax.random.fold_in(own_key, 3), rows)[jnp.arange(count) % rows]
    lots = jnp.where(jnp.arange(rows)[:, None] == fixed_rows[None, :], 1 << 14, lots)
    score = lots * count + jnp.arange(count)
    return lax.top_k(score.astype(jnp.int32), top)[1].astype(jnp.int32)


def profile(count, total, limit, skew):
    portions = [(1 << 20) // math.isqrt(grade ** skew) + 1 for grade in range(2, count + 1)]
    spare, counts = total - limit - (count - 1), [1] * (count - 1)
    while spare > 0:
        free = [i for i in range(count - 1) if counts[i] < limit]
        pool, left = sum([portions[i] for i in free]), spare
        for i in free:
            more = min(limit - counts[i], max(1, left * portions[i] // pool), spare)
            counts[i] = counts[i] + more
            spare = spare - more
    return np.array([limit] + counts)


def ragged_sizes(key, amount, total, bound, lean):
    if amount == 2:
        one = jax.random.randint(key, (), max(1, total - bound), min(bound, total - 1) + 1)
        return jnp.stack([one, total - one])
    tallies = jnp.asarray(profile(amount, total, bound, lean), jnp.int32)
    couples = (amount - 1) // 2
    giver, sink = tallies[1:1 + 2 * couples:2], tallies[2:2 + 2 * couples:2]
    margin = jnp.minimum(giver - 1, bound - sink)
    shifted = jax.random.randint(jax.random.fold_in(key, 1), (couples,), 0, 1 << 20) % (margin + 1)
    tallies = tallies.at[1:1 + 2 * couples:2].set(giver - shifted).at[2:2 + 2 * couples:2].set(sink + shifted)
    return tallies[jax.random.permutation(jax.random.fold_in(key, 2), amount)]


def noise(rng, shape, deviation, reach, pieces=(), held_as=jnp.bfloat16):
    array = deviation * jax.random.normal(rng, shape, jnp.float32)
    if pieces:
        array = array * levels(rng, shape, pieces, -0.22, 0.18)
    return jnp.clip(array, -reach, reach).astype(held_as)


def setup_inputs(seed: int = 0) -> dict:
    seeds = jax.random.split(jax.random.key(seed), 7)
    layer_in = draw_layer_in(jax.random.fold_in(seeds[6], 71), 0)
    kv_in = draw_kv_in(jax.random.fold_in(seeds[6], 71), 0)
    out_grad = noise(seeds[2], (DOCUMENT_TOKENS, QUERY_HEADS * HEAD_SIZE), 1.0, 6.0, ((0, 64), (1, 8)))
    sentences = jnp.searchsorted(jnp.cumsum(ragged_sizes(seeds[3], DOCUMENT_TOKENS // 32, DOCUMENT_TOKENS, min(96, DOCUMENT_TOKENS // 2), 2)), jnp.arange(DOCUMENT_TOKENS), side="right").astype(jnp.int32)
    anchor_blocks = draw_anchor_blocks(jax.random.fold_in(seeds[6], 71), 0)
    anchor_pick = choose_distinct(seeds[5], NBLK, NANCH, APICK, 0)
    return {"layer_in": layer_in, "kv_in": kv_in, "out_grad": out_grad, "sentences": sentences, "anchor_blocks": anchor_blocks, "anchor_pick": anchor_pick}


def layer_back(query_rows, keyvals, cot, sentences, anchor_blocks, picks):
    tok = query_rows.shape[0]
    nblk = tok // BLK
    kvh = keyvals.shape[1] // (2 * HEAD_SIZE)
    group_size = query_rows.shape[1] // (kvh * HEAD_SIZE)
    feat = keyvals.shape[1]
    scale = HEAD_SIZE ** -0.5
    q_blocks = query_rows.reshape(nblk, BLK, kvh, group_size, HEAD_SIZE)
    kv_blocks = keyvals.reshape(nblk, BLK, kvh, 2, HEAD_SIZE)
    c_blocks = cot.reshape(nblk, BLK, kvh, group_size, HEAD_SIZE)
    s_blocks = sentences.reshape(nblk, BLK)
    anchors = kv_blocks[anchor_blocks]
    index_all = jnp.arange(nblk, dtype=jnp.int32)
    idx = jnp.arange(BLK, dtype=jnp.int32)
    choose = jnp.arange(NANCH, dtype=jnp.int32)

    def step(acc, item):
        qv, kv, cv, sent, pick, index = item
        far = anchors[pick].reshape(APICK * BLK, kvh, 2, HEAD_SIZE)
        keys = jnp.concatenate([kv, far], axis=0).astype(jnp.float32)
        kk = keys[:, :, 0]
        vv = keys[:, :, 1]
        qf = qv.astype(jnp.float32)
        cf = cv.astype(jnp.float32)
        score = jnp.einsum('qkgd,lkd->kgql', qf, kk) * scale
        band = (idx[None, :] <= idx[:, None]) & (sent[:, None] == sent[None, :])
        valid = jnp.repeat(anchor_blocks[pick] < index, BLK)
        mask = jnp.concatenate([band, jnp.broadcast_to(valid[None, :], (BLK, APICK * BLK))], axis=1)
        score = jnp.where(mask[None, None], score, jnp.float32(-1e30))
        top = jnp.max(score, axis=-1, keepdims=True)
        expo = jnp.exp(score - top)
        probs = expo / jnp.sum(expo, axis=-1, keepdims=True)
        pb = probs.astype(jnp.bfloat16).astype(jnp.float32)
        outp = jnp.einsum('kgql,lkd->qkgd', pb, vv)
        delta = jnp.sum(cf * outp, axis=-1).transpose(1, 2, 0)[..., None]
        dprob = jnp.einsum('qkgd,lkd->kgql', cf, vv)
        dscore = (probs * (dprob - delta)).astype(jnp.bfloat16).astype(jnp.float32)
        dq = jnp.einsum('kgql,lkd->qkgd', dscore, kk) * scale
        dk = jnp.einsum('kgql,qkgd->lkd', dscore, qf) * scale
        dv = jnp.einsum('kgql,qkgd->lkd', pb, cf)
        dkv = jnp.stack([dk, dv], axis=2)
        band_grad = dkv[:BLK].reshape(BLK, feat)
        far_grad = dkv[BLK:].reshape(APICK, BLK * feat)
        onehot = (pick[:, None] == choose[None, :]).astype(jnp.float32)
        acc = acc + jnp.dot(onehot.T, far_grad, precision=lax.Precision.HIGHEST).reshape(NANCH, BLK, feat)
        return acc, (dq.reshape(BLK, -1), band_grad)

    init = jnp.zeros((NANCH, BLK, feat), jnp.float32)
    acc, (dq, band) = lax.scan(step, init, (q_blocks, kv_blocks, c_blocks, s_blocks, picks, index_all))
    band = band.at[anchor_blocks].add(acc)
    return dq.reshape(tok, -1), band.reshape(tok, feat)


def reference(layer_in, kv_in, out_grad, sentences, anchor_blocks, anchor_pick):
    dq_two, dkv_two = layer_back(layer_in[1], kv_in[1], out_grad, sentences, anchor_blocks, anchor_pick)
    sent_back = dq_two.astype(jnp.bfloat16)
    dq_one, dkv_one = layer_back(layer_in[0], kv_in[0], sent_back, sentences, anchor_blocks, anchor_pick)
    input_grad = jnp.stack([dq_one.astype(jnp.bfloat16), sent_back])
    kv_grad = jnp.stack([dkv_one.astype(jnp.bfloat16), dkv_two.astype(jnp.bfloat16)])
    return input_grad, kv_grad
```

```python
import jax
import jax.numpy as jnp
from jax import lax
from jax.sharding import PartitionSpec as P

HEAD_SIZE = 128
BLK = 128


def from_behind(x, axis, by):
    peers = lax.axis_size(axis)
    pairs = [(i, i + by) for i in range(peers) if 0 <= i + by < peers]
    return lax.ppermute(x, axis, pairs)


def swap(x, axis, bit):
    peers = lax.axis_size(axis)
    return lax.ppermute(x, axis, [(i, i ^ bit) for i in range(peers)])


def attend(query_rows, keyvals, anchor_kv, cot, sentences, picks, anchor_blocks, blocks):
    rows, width = query_rows.shape
    feat = keyvals.shape[1]
    kvh = feat // (2 * HEAD_SIZE)
    group_size = width // (kvh * HEAD_SIZE)
    per_dev = rows // BLK
    npick = picks.shape[1]
    nanch = anchor_kv.shape[0]
    scale = HEAD_SIZE ** (-0.5)
    q_blocks = query_rows.reshape(per_dev, BLK, kvh, group_size, HEAD_SIZE)
    own = keyvals.reshape(per_dev, BLK, kvh, 2, HEAD_SIZE)
    far = anchor_kv.reshape(nanch, BLK, kvh, 2, HEAD_SIZE)[picks].reshape(
        per_dev, npick * BLK, kvh, 2, HEAD_SIZE
    )
    keys = jnp.concatenate([own, far], axis=1)
    kk = keys[:, :, :, 0]
    vv = keys[:, :, :, 1]
    score = (
        jnp.einsum("bqkgd,blkd->bkgql", q_blocks, kk, preferred_element_type=jnp.float32) * scale
    )
    sent = sentences.reshape(per_dev, BLK)
    idx = jnp.arange(BLK, dtype=jnp.int32)
    band = (idx[None, :, None] >= idx[None, None, :]) & (sent[:, :, None] == sent[:, None, :])
    valid = jnp.repeat(anchor_blocks[picks] < blocks[:, None], BLK, axis=1)
    far_mask = jnp.broadcast_to(valid[:, None, :], (per_dev, BLK, npick * BLK))
    mask = jnp.concatenate([band, far_mask], axis=2)[:, None, None]
    score = jnp.where(mask, score, jnp.float32(-1e30))
    top = jnp.max(score, axis=-1, keepdims=True)
    expo = jnp.exp(score - top)
    probs = expo / jnp.sum(expo, axis=-1, keepdims=True)
    pb = probs.astype(jnp.bfloat16)
    outp = jnp.einsum("bkgql,blkd->bqkgd", pb, vv, preferred_element_type=jnp.float32)
    c_blocks = cot.reshape(per_dev, BLK, kvh, group_size, HEAD_SIZE)
    delta = jnp.sum(c_blocks.astype(jnp.float32) * outp, axis=-1).transpose(0, 2, 3, 1)[..., None]
    dprob = jnp.einsum("bqkgd,blkd->bkgql", c_blocks, vv, preferred_element_type=jnp.float32)
    dscore = (probs * (dprob - delta)).astype(jnp.bfloat16)
    dq = jnp.einsum("bkgql,blkd->bqkgd", dscore, kk, preferred_element_type=jnp.float32) * scale
    dk = (
        jnp.einsum("bkgql,bqkgd->blkd", dscore, q_blocks, preferred_element_type=jnp.float32)
        * scale
    )
    dv = jnp.einsum("bkgql,bqkgd->blkd", pb, c_blocks, preferred_element_type=jnp.float32)
    dkv = jnp.stack([dk, dv], axis=3)
    band_grad = dkv[:, :BLK].reshape(rows, feat)
    far_grad = dkv[:, BLK:].reshape(per_dev, npick, BLK * feat)
    onehot = (picks[:, :, None] == jnp.arange(nanch, dtype=jnp.int32)[None, None, :]).astype(
        jnp.float32
    )
    anchor_term = jnp.einsum("ban,bam->nm", onehot, far_grad, precision=lax.Precision.HIGHEST)
    return (dq.reshape(rows, width), band_grad, anchor_term.reshape(nanch, BLK, feat))


def spread_anchors(mine, span, nanch, rank):
    bit = 1
    while bit < span:
        mine = mine + swap(mine, "ctx", bit)
        bit *= 2
    got = mine[None]
    bit = 1
    while bit < nanch:
        other = swap(got, "ctx", bit * span)
        lower = (rank & bit) == 0
        got = jnp.where(
            lower, jnp.concatenate([got, other], axis=0), jnp.concatenate([other, got], axis=0)
        )
        bit *= 2
    return got


def gather_grads(acc, span, nanch, rank):
    size = nanch
    bit = nanch // 2
    while bit >= 1:
        half = size // 2
        upper = (rank & bit) != 0
        lo, hi = acc[:half], acc[half:]
        keep = jnp.where(upper, hi, lo)
        send = jnp.where(upper, lo, hi)
        acc = keep + swap(send, "ctx", bit * span)
        size = half
        bit //= 2
    bit = 1
    while bit < span:
        acc = acc + swap(acc, "ctx", bit)
        bit *= 2
    return acc[0]


def body(layer_in, kv_in, out_grad, sentences, anchor_blocks, anchor_pick):
    query_rows = layer_in[0]
    keyvals = kv_in[0]
    rows, width = query_rows.shape
    feat = keyvals.shape[1]
    per_dev = rows // BLK
    nanch = anchor_blocks.shape[0]
    span = lax.axis_size("ctx") // nanch
    ctx = lax.axis_index("ctx")
    rank = ctx // span
    section_one = lax.axis_index("section") == 1
    blocks = ctx * per_dev + jnp.arange(per_dev, dtype=jnp.int32)
    kv_blocks = keyvals.reshape(per_dev, BLK, feat)
    hit = anchor_blocks[None, :] == blocks[:, None]
    holder = jnp.sum(hit.astype(jnp.float32), axis=1).astype(jnp.bfloat16)
    mine = jnp.einsum("b,bmf->mf", holder, kv_blocks, preferred_element_type=jnp.float32).astype(
        jnp.bfloat16
    )
    anchor_kv = spread_anchors(mine, span, nanch, rank)
    dq_first, band_first, term_first = attend(
        query_rows, keyvals, anchor_kv, out_grad, sentences, anchor_pick, anchor_blocks, blocks
    )
    sent_back = dq_first.astype(jnp.bfloat16)
    arrived = from_behind(sent_back, "section", -1)
    dq_second, band_second, term_second = attend(
        query_rows, keyvals, anchor_kv, arrived, sentences, anchor_pick, anchor_blocks, blocks
    )
    band_grad = jnp.where(section_one, band_first, band_second)
    anchor_term = jnp.where(section_one, term_first, term_second)
    total = gather_grads(anchor_term, span, nanch, rank)
    owner = (anchor_blocks[rank] == blocks).astype(jnp.float32)
    owned = owner[:, None, None] * total[None]
    kv_grad = (band_grad + owned.reshape(band_grad.shape)).astype(jnp.bfloat16)
    input_grad = jnp.where(section_one, sent_back, dq_second.astype(jnp.bfloat16))
    return (input_grad[None], kv_grad[None])


def solution(mesh):
    placed = (
        P("section", "ctx", "head"),
        P("section", "ctx", "head"),
        P("ctx", "head"),
        P("ctx"),
        P(),
        P("ctx", None),
    )
    return jax.shard_map(
        body,
        mesh=mesh,
        in_specs=placed,
        out_specs=(P("section", "ctx", "head"), P("section", "ctx", "head")),
        check_vma=False,
    )
```

```python
import jax
import jax.numpy as jnp
from jax import lax
from jax.sharding import Mesh, PartitionSpec as P

HEAD_SIZE = 128
BLK = 128


def from_behind(x, axis, by):
    peers = lax.axis_size(axis)
    pairs = [(i, i + by) for i in range(peers) if 0 <= i + by < peers]
    return lax.ppermute(x, axis, pairs)


def attend(query_rows, keyvals, anchor_kv, cot, sentences, picks, anchor_blocks, blocks):
    rows, width = query_rows.shape
    feat = keyvals.shape[1]
    kvh = feat // (2 * HEAD_SIZE)
    group_size = width // (kvh * HEAD_SIZE)
    per_dev = rows // BLK
    npick = picks.shape[1]
    nanch = anchor_kv.shape[0]
    scale = HEAD_SIZE ** (-0.5)
    q_blocks = query_rows.reshape(per_dev, BLK, kvh, group_size, HEAD_SIZE)
    own = keyvals.reshape(per_dev, BLK, kvh, 2, HEAD_SIZE)
    far = anchor_kv.reshape(nanch, BLK, kvh, 2, HEAD_SIZE)[picks].reshape(
        per_dev, npick * BLK, kvh, 2, HEAD_SIZE
    )
    keys = jnp.concatenate([own, far], axis=1)
    kk = keys[:, :, :, 0]
    vv = keys[:, :, :, 1]
    score = (
        jnp.einsum("bqkgd,blkd->bkgql", q_blocks, kk, preferred_element_type=jnp.float32) * scale
    )
    sent = sentences.reshape(per_dev, BLK)
    idx = jnp.arange(BLK, dtype=jnp.int32)
    band = (idx[None, :, None] >= idx[None, None, :]) & (sent[:, :, None] == sent[:, None, :])
    valid = jnp.repeat(anchor_blocks[picks] < blocks[:, None], BLK, axis=1)
    far_mask = jnp.broadcast_to(valid[:, None, :], (per_dev, BLK, npick * BLK))
    mask = jnp.concatenate([band, far_mask], axis=2)[:, None, None]
    score = jnp.where(mask, score, jnp.float32(-1e30))
    top = jnp.max(score, axis=-1, keepdims=True)
    expo = jnp.exp(score - top)
    probs = expo / jnp.sum(expo, axis=-1, keepdims=True)
    pb = probs.astype(jnp.bfloat16)
    outp = jnp.einsum("bkgql,blkd->bqkgd", pb, vv, preferred_element_type=jnp.float32)
    c_blocks = cot.reshape(per_dev, BLK, kvh, group_size, HEAD_SIZE)
    delta = jnp.sum(c_blocks.astype(jnp.float32) * outp, axis=-1).transpose(0, 2, 3, 1)[..., None]
    dprob = jnp.einsum("bqkgd,blkd->bkgql", c_blocks, vv, preferred_element_type=jnp.float32)
    dscore = (probs * (dprob - delta)).astype(jnp.bfloat16)
    dq = jnp.einsum("bkgql,blkd->bqkgd", dscore, kk, preferred_element_type=jnp.float32) * scale
    dk = (
        jnp.einsum("bkgql,bqkgd->blkd", dscore, q_blocks, preferred_element_type=jnp.float32)
        * scale
    )
    dv = jnp.einsum("bkgql,bqkgd->blkd", pb, c_blocks, preferred_element_type=jnp.float32)
    dkv = jnp.stack([dk, dv], axis=3)
    band_grad = dkv[:, :BLK].reshape(rows, feat)
    far_grad = dkv[:, BLK:].reshape(per_dev, npick, BLK * feat)
    onehot = (picks[:, :, None] == jnp.arange(nanch, dtype=jnp.int32)[None, None, :]).astype(
        jnp.float32
    )
    anchor_term = jnp.einsum("ban,bam->nm", onehot, far_grad, precision=lax.Precision.HIGHEST)
    return (dq.reshape(rows, width), band_grad, anchor_term.reshape(nanch, BLK, feat))


def spread_anchors(mine, rows_per_slot):
    ny = lax.axis_size("cy")
    nx = lax.axis_size("cx")
    blk, feat = mine.shape
    part = mine.reshape(ny, blk // ny, feat)
    got = lax.all_to_all(part, "cy", 0, 0, tiled=True)
    row = jnp.sum(got.astype(jnp.float32), axis=0).astype(mine.dtype)
    got = lax.all_to_all(jnp.broadcast_to(row[None], (nx,) + row.shape), "cx", 0, 0, tiled=True)
    nslot = nx // rows_per_slot
    slots = jnp.sum(
        got.reshape(nslot, rows_per_slot, *row.shape).astype(jnp.float32), axis=1
    ).astype(mine.dtype)
    got = lax.all_to_all(jnp.broadcast_to(slots[None], (ny,) + slots.shape), "cy", 0, 0, tiled=True)
    return got.transpose(1, 0, 2, 3).reshape(nslot, blk, feat)


def gather_grads(acc, rows_per_slot):
    ny = lax.axis_size("cy")
    nslot, blk, feat = acc.shape
    part = acc.reshape(nslot, ny, blk // ny, feat).transpose(1, 0, 2, 3)
    got = lax.all_to_all(part, "cy", 0, 0, tiled=True)
    rowsum = jnp.sum(got, axis=0)
    got = lax.all_to_all(jnp.repeat(rowsum, rows_per_slot, axis=0), "cx", 0, 0, tiled=True)
    total = jnp.sum(got, axis=0)
    got = lax.all_to_all(jnp.broadcast_to(total[None], (ny,) + total.shape), "cy", 0, 0, tiled=True)
    return got.reshape(blk, feat)


def body(layer_in, kv_in, out_grad, sentences, anchor_blocks, anchor_pick):
    query_rows = layer_in[0]
    keyvals = kv_in[0]
    rows, width = query_rows.shape
    feat = keyvals.shape[1]
    per_dev = rows // BLK
    nanch = anchor_blocks.shape[0]
    rows_per_slot = lax.axis_size("cx") // nanch
    ctx = lax.axis_index("cx") * lax.axis_size("cy") + lax.axis_index("cy")
    rank = lax.axis_index("cx") // rows_per_slot
    section_one = lax.axis_index("section") == 1
    blocks = ctx * per_dev + jnp.arange(per_dev, dtype=jnp.int32)
    kv_blocks = keyvals.reshape(per_dev, BLK, feat)
    hit = anchor_blocks[None, :] == blocks[:, None]
    holder = jnp.sum(hit.astype(jnp.float32), axis=1).astype(jnp.bfloat16)
    mine = jnp.einsum("b,bmf->mf", holder, kv_blocks, preferred_element_type=jnp.float32).astype(
        jnp.bfloat16
    )
    anchor_kv = spread_anchors(mine, rows_per_slot)
    dq_first, band_first, term_first = attend(
        query_rows, keyvals, anchor_kv, out_grad, sentences, anchor_pick, anchor_blocks, blocks
    )
    sent_back = dq_first.astype(jnp.bfloat16)
    arrived = from_behind(sent_back, "section", -1)
    dq_second, band_second, term_second = attend(
        query_rows, keyvals, anchor_kv, arrived, sentences, anchor_pick, anchor_blocks, blocks
    )
    band_grad = jnp.where(section_one, band_first, band_second)
    anchor_term = jnp.where(section_one, term_first, term_second)
    total = gather_grads(anchor_term, rows_per_slot)
    owner = (anchor_blocks[rank] == blocks).astype(jnp.float32)
    owned = owner[:, None, None] * total[None]
    kv_grad = (band_grad + owned.reshape(band_grad.shape)).astype(jnp.bfloat16)
    input_grad = jnp.where(section_one, sent_back, dq_second.astype(jnp.bfloat16))
    return (input_grad[None], kv_grad[None])


def solution(mesh):
    ny = 8
    devs = mesh.devices
    grid = Mesh(
        devs.reshape(devs.shape[0], devs.shape[1] // ny, ny, devs.shape[2]),
        ("section", "cx", "cy", "head"),
    )
    ctx = ("cx", "cy")
    placed = (
        P("section", ctx, "head"),
        P("section", ctx, "head"),
        P(ctx, "head"),
        P(ctx),
        P(),
        P(ctx, None),
    )
    return jax.shard_map(
        body,
        mesh=grid,
        in_specs=placed,
        out_specs=(P("section", ctx, "head"), P("section", ctx, "head")),
        check_vma=False,
    )
```

```python
import jax
import jax.numpy as jnp
from jax import lax
from jax.sharding import Mesh, PartitionSpec as P

HEAD_SIZE = 128
BLK = 128


def from_behind(x, axis, by):
    peers = lax.axis_size(axis)
    pairs = [(i, i + by) for i in range(peers) if 0 <= i + by < peers]
    return lax.ppermute(x, axis, pairs)


def attend(query_rows, keyvals, anchor_kv, cot, sentences, picks, anchor_blocks, blocks):
    rows, width = query_rows.shape
    feat = keyvals.shape[1]
    kvh = feat // (2 * HEAD_SIZE)
    group_size = width // (kvh * HEAD_SIZE)
    per_dev = rows // BLK
    npick = picks.shape[1]
    nanch = anchor_kv.shape[0]
    scale = HEAD_SIZE ** (-0.5)
    q_blocks = query_rows.reshape(per_dev, BLK, kvh, group_size, HEAD_SIZE)
    own = keyvals.reshape(per_dev, BLK, kvh, 2, HEAD_SIZE)
    far = anchor_kv.reshape(nanch, BLK, kvh, 2, HEAD_SIZE)[picks].reshape(
        per_dev, npick * BLK, kvh, 2, HEAD_SIZE
    )
    keys = jnp.concatenate([own, far], axis=1)
    kk = keys[:, :, :, 0]
    vv = keys[:, :, :, 1]
    score = (
        jnp.einsum("bqkgd,blkd->bkgql", q_blocks, kk, preferred_element_type=jnp.float32) * scale
    )
    sent = sentences.reshape(per_dev, BLK)
    idx = jnp.arange(BLK, dtype=jnp.int32)
    band = (idx[None, :, None] >= idx[None, None, :]) & (sent[:, :, None] == sent[:, None, :])
    valid = jnp.repeat(anchor_blocks[picks] < blocks[:, None], BLK, axis=1)
    far_mask = jnp.broadcast_to(valid[:, None, :], (per_dev, BLK, npick * BLK))
    mask = jnp.concatenate([band, far_mask], axis=2)[:, None, None]
    score = jnp.where(mask, score, jnp.float32(-1e30))
    top = jnp.max(score, axis=-1, keepdims=True)
    expo = jnp.exp(score - top)
    probs = expo / jnp.sum(expo, axis=-1, keepdims=True)
    pb = probs.astype(jnp.bfloat16)
    outp = jnp.einsum("bkgql,blkd->bqkgd", pb, vv, preferred_element_type=jnp.float32)
    c_blocks = cot.reshape(per_dev, BLK, kvh, group_size, HEAD_SIZE)
    delta = jnp.sum(c_blocks.astype(jnp.float32) * outp, axis=-1).transpose(0, 2, 3, 1)[..., None]
    dprob = jnp.einsum("bqkgd,blkd->bkgql", c_blocks, vv, preferred_element_type=jnp.float32)
    dscore = (probs * (dprob - delta)).astype(jnp.bfloat16)
    dq = jnp.einsum("bkgql,blkd->bqkgd", dscore, kk, preferred_element_type=jnp.float32) * scale
    dk = (
        jnp.einsum("bkgql,bqkgd->blkd", dscore, q_blocks, preferred_element_type=jnp.float32)
        * scale
    )
    dv = jnp.einsum("bkgql,bqkgd->blkd", pb, c_blocks, preferred_element_type=jnp.float32)
    dkv = jnp.stack([dk, dv], axis=3)
    band_grad = dkv[:, :BLK].reshape(rows, feat)
    far_grad = dkv[:, BLK:].reshape(per_dev * npick, BLK, feat)
    return (dq.reshape(rows, width), band_grad, far_grad)


def spread_anchors(mine, rows_per_slot):
    ny = lax.axis_size("cy")
    nx = lax.axis_size("cx")
    blk, feat = mine.shape
    part = mine.reshape(ny, blk // ny, feat)
    got = lax.all_to_all(part, "cy", 0, 0, tiled=True)
    row = jnp.sum(got.astype(jnp.float32), axis=0).astype(mine.dtype)
    got = lax.all_to_all(jnp.broadcast_to(row[None], (nx,) + row.shape), "cx", 0, 0, tiled=True)
    nslot = nx // rows_per_slot
    slots = jnp.sum(
        got.reshape(nslot, rows_per_slot, *row.shape).astype(jnp.float32), axis=1
    ).astype(mine.dtype)
    got = lax.all_to_all(jnp.broadcast_to(slots[None], (ny,) + slots.shape), "cy", 0, 0, tiled=True)
    return got.transpose(1, 0, 2, 3).reshape(nslot, blk, feat)


def gather_grads(far, picks, nslot, rows_per_slot):
    ny = lax.axis_size("cy")
    npick, blk, feat = far.shape
    size = (blk // ny) * feat
    data = far.reshape(npick, ny, size)
    tag = jnp.broadcast_to(picks.astype(jnp.float32)[:, None, None], (npick, ny, 128))
    load = jnp.concatenate([data, tag], axis=2).transpose(1, 0, 2)
    got = lax.all_to_all(load, "cy", 0, 0, tiled=True)
    vals = got[:, :, :size]
    ids = got[:, :, size]
    slot_ids = jnp.arange(nslot, dtype=jnp.float32)
    rowsum = jnp.sum(
        jnp.where(ids[None, :, :, None] == slot_ids[:, None, None, None], vals[None], 0.0),
        axis=(1, 2),
    ).reshape(nslot, blk // ny, feat)
    got = lax.all_to_all(jnp.repeat(rowsum, rows_per_slot, axis=0), "cx", 0, 0, tiled=True)
    total = jnp.sum(got, axis=0)
    got = lax.all_to_all(jnp.broadcast_to(total[None], (ny,) + total.shape), "cy", 0, 0, tiled=True)
    return got.reshape(blk, feat)


def body(layer_in, kv_in, out_grad, sentences, anchor_blocks, anchor_pick):
    query_rows = layer_in[0]
    keyvals = kv_in[0]
    rows, width = query_rows.shape
    feat = keyvals.shape[1]
    per_dev = rows // BLK
    nanch = anchor_blocks.shape[0]
    rows_per_slot = lax.axis_size("cx") // nanch
    ctx = lax.axis_index("cx") * lax.axis_size("cy") + lax.axis_index("cy")
    rank = lax.axis_index("cx") // rows_per_slot
    section_one = lax.axis_index("section") == 1
    blocks = ctx * per_dev + jnp.arange(per_dev, dtype=jnp.int32)
    kv_blocks = keyvals.reshape(per_dev, BLK, feat)
    hit = anchor_blocks[None, :] == blocks[:, None]
    holder = jnp.sum(hit.astype(jnp.float32), axis=1).astype(jnp.bfloat16)
    mine = jnp.einsum("b,bmf->mf", holder, kv_blocks, preferred_element_type=jnp.float32).astype(
        jnp.bfloat16
    )
    anchor_kv = spread_anchors(mine, rows_per_slot)
    npick = anchor_pick.shape[1]

    def run(cot):
        return attend(
            query_rows, keyvals, anchor_kv, cot, sentences, anchor_pick, anchor_blocks, blocks
        )

    def idle(cot):
        return (
            jnp.zeros((rows, query_rows.shape[1]), jnp.float32),
            jnp.zeros((rows, feat), jnp.float32),
            jnp.zeros((per_dev * npick, BLK, feat), jnp.float32),
        )

    dq_first, band_first, far_first = lax.cond(section_one, run, idle, out_grad)
    sent_back = dq_first.astype(jnp.bfloat16)
    arrived = from_behind(sent_back, "section", -1)
    dq_second, band_second, far_second = lax.cond(section_one, idle, run, arrived)
    band_grad = jnp.where(section_one, band_first, band_second)
    far = jnp.where(section_one, far_first, far_second)
    total = gather_grads(far, anchor_pick.reshape(-1), nanch, rows_per_slot)
    owner = (anchor_blocks[rank] == blocks).astype(jnp.float32)
    owned = owner[:, None, None] * total[None]
    kv_grad = (band_grad + owned.reshape(band_grad.shape)).astype(jnp.bfloat16)
    input_grad = jnp.where(section_one, sent_back, dq_second.astype(jnp.bfloat16))
    return (input_grad[None], kv_grad[None])


def solution(mesh):
    ny = 8
    devs = mesh.devices
    grid = Mesh(
        devs.reshape(devs.shape[0], devs.shape[1] // ny, ny, devs.shape[2]),
        ("section", "cx", "cy", "head"),
    )
    ctx = ("cx", "cy")
    placed = (
        P("section", ctx, "head"),
        P("section", ctx, "head"),
        P(ctx, "head"),
        P(ctx),
        P(),
        P(ctx, None),
    )
    return jax.shard_map(
        body,
        mesh=grid,
        in_specs=placed,
        out_specs=(P("section", ctx, "head"), P("section", ctx, "head")),
        check_vma=False,
    )
```

```python
import jax
import jax.numpy as jnp
from jax import lax
from jax.sharding import Mesh, PartitionSpec as P

HEAD_SIZE = 128
BLK = 128


def from_behind(x, axis, by):
    peers = lax.axis_size(axis)
    pairs = [(i, i + by) for i in range(peers) if 0 <= i + by < peers]
    return lax.ppermute(x, axis, pairs)


def gather_keys(keyvals, anchor_kv, picks):
    rows, feat = keyvals.shape
    kvh = feat // (2 * HEAD_SIZE)
    per_dev = rows // BLK
    npick = picks.shape[1]
    nanch = anchor_kv.shape[0]
    own = keyvals.reshape(per_dev, BLK, kvh, 2, HEAD_SIZE)
    far = anchor_kv.reshape(nanch, BLK, kvh, 2, HEAD_SIZE)[picks].reshape(
        per_dev, npick * BLK, kvh, 2, HEAD_SIZE
    )
    keys = jnp.concatenate([own, far], axis=1)
    return keys[:, :, :, 0], keys[:, :, :, 1]


def forward(query_rows, kk, sentences, picks, anchor_blocks, blocks):
    rows, width = query_rows.shape
    kvh = kk.shape[2]
    group_size = width // (kvh * HEAD_SIZE)
    per_dev = rows // BLK
    npick = picks.shape[1]
    scale = HEAD_SIZE ** (-0.5)
    q_blocks = query_rows.reshape(per_dev, BLK, kvh, group_size, HEAD_SIZE)
    score = (
        jnp.einsum("bqkgd,blkd->bkgql", q_blocks, kk, preferred_element_type=jnp.float32) * scale
    )
    sent = sentences.reshape(per_dev, BLK)
    idx = jnp.arange(BLK, dtype=jnp.int32)
    band = (idx[None, :, None] >= idx[None, None, :]) & (sent[:, :, None] == sent[:, None, :])
    valid = jnp.repeat(anchor_blocks[picks] < blocks[:, None], BLK, axis=1)
    far_mask = jnp.broadcast_to(valid[:, None, :], (per_dev, BLK, npick * BLK))
    mask = jnp.concatenate([band, far_mask], axis=2)[:, None, None]
    score = jnp.where(mask, score, jnp.float32(-1e30))
    top = jnp.max(score, axis=-1, keepdims=True)
    expo = jnp.exp(score - top)
    return expo / jnp.sum(expo, axis=-1, keepdims=True)


def backward(query_rows, kk, vv, probs, cot):
    rows, width = query_rows.shape
    kvh = kk.shape[2]
    feat = 2 * kvh * HEAD_SIZE
    group_size = width // (kvh * HEAD_SIZE)
    per_dev = rows // BLK
    scale = HEAD_SIZE ** (-0.5)
    q_blocks = query_rows.reshape(per_dev, BLK, kvh, group_size, HEAD_SIZE)
    pb = probs.astype(jnp.bfloat16)
    outp = jnp.einsum("bkgql,blkd->bqkgd", pb, vv, preferred_element_type=jnp.float32)
    c_blocks = cot.reshape(per_dev, BLK, kvh, group_size, HEAD_SIZE)
    delta = jnp.sum(c_blocks.astype(jnp.float32) * outp, axis=-1).transpose(0, 2, 3, 1)[..., None]
    dprob = jnp.einsum("bqkgd,blkd->bkgql", c_blocks, vv, preferred_element_type=jnp.float32)
    dscore = (probs * (dprob - delta)).astype(jnp.bfloat16)
    dq = jnp.einsum("bkgql,blkd->bqkgd", dscore, kk, preferred_element_type=jnp.float32) * scale
    dk = (
        jnp.einsum("bkgql,bqkgd->blkd", dscore, q_blocks, preferred_element_type=jnp.float32)
        * scale
    )
    dv = jnp.einsum("bkgql,bqkgd->blkd", pb, c_blocks, preferred_element_type=jnp.float32)
    dkv = jnp.stack([dk, dv], axis=3)
    band_grad = dkv[:, :BLK].reshape(rows, feat)
    far_grad = dkv[:, BLK:].reshape(-1, BLK, feat)
    return (dq.reshape(rows, width), band_grad, far_grad)


def spread_anchors(mine, rows_per_slot):
    ny = lax.axis_size("cy")
    nx = lax.axis_size("cx")
    blk, feat = mine.shape
    part = mine.reshape(ny, blk // ny, feat)
    got = lax.all_to_all(part, "cy", 0, 0, tiled=True)
    row = jnp.sum(got.astype(jnp.float32), axis=0).astype(mine.dtype)
    got = lax.all_to_all(jnp.broadcast_to(row[None], (nx,) + row.shape), "cx", 0, 0, tiled=True)
    nslot = nx // rows_per_slot
    slots = jnp.sum(
        got.reshape(nslot, rows_per_slot, *row.shape).astype(jnp.float32), axis=1
    ).astype(mine.dtype)
    got = lax.all_to_all(jnp.broadcast_to(slots[None], (ny,) + slots.shape), "cy", 0, 0, tiled=True)
    return got.transpose(1, 0, 2, 3).reshape(nslot, blk, feat)


def gather_grads(far, picks, nslot, rows_per_slot):
    ny = lax.axis_size("cy")
    npick, blk, feat = far.shape
    size = (blk // ny) * feat
    data = far.reshape(npick, ny, size)
    tag = jnp.broadcast_to(picks.astype(jnp.float32)[:, None, None], (npick, ny, 128))
    load = jnp.concatenate([data, tag], axis=2).transpose(1, 0, 2)
    got = lax.all_to_all(load, "cy", 0, 0, tiled=True)
    vals = got[:, :, :size]
    ids = got[:, :, size]
    slot_ids = jnp.arange(nslot, dtype=jnp.float32)
    rowsum = jnp.sum(
        jnp.where(ids[None, :, :, None] == slot_ids[:, None, None, None], vals[None], 0.0),
        axis=(1, 2),
    ).reshape(nslot, blk // ny, feat)
    got = lax.all_to_all(jnp.repeat(rowsum, rows_per_slot, axis=0), "cx", 0, 0, tiled=True)
    total = jnp.sum(got, axis=0)
    got = lax.all_to_all(jnp.broadcast_to(total[None], (ny,) + total.shape), "cy", 0, 0, tiled=True)
    return got.reshape(blk, feat)


def body(layer_in, kv_in, out_grad, sentences, anchor_blocks, anchor_pick):
    query_rows = layer_in[0]
    keyvals = kv_in[0]
    rows, width = query_rows.shape
    feat = keyvals.shape[1]
    per_dev = rows // BLK
    nanch = anchor_blocks.shape[0]
    rows_per_slot = lax.axis_size("cx") // nanch
    ctx = lax.axis_index("cx") * lax.axis_size("cy") + lax.axis_index("cy")
    rank = lax.axis_index("cx") // rows_per_slot
    section_one = lax.axis_index("section") == 1
    blocks = ctx * per_dev + jnp.arange(per_dev, dtype=jnp.int32)
    kv_blocks = keyvals.reshape(per_dev, BLK, feat)
    hit = anchor_blocks[None, :] == blocks[:, None]
    holder = jnp.any(hit, axis=1)[:, None, None]
    mine = jnp.where(holder, kv_blocks, jnp.zeros_like(kv_blocks)).sum(axis=0, dtype=jnp.float32)
    mine = mine.astype(jnp.bfloat16)
    anchor_kv = spread_anchors(mine, rows_per_slot)
    npick = anchor_pick.shape[1]
    kk, vv = gather_keys(keyvals, anchor_kv, anchor_pick)

    def zeros():
        return (
            jnp.zeros((rows, query_rows.shape[1]), jnp.float32),
            jnp.zeros((rows, feat), jnp.float32),
            jnp.zeros((per_dev * npick, BLK, feat), jnp.float32),
        )

    def probs_of():
        return forward(query_rows, kk, sentences, anchor_pick, anchor_blocks, blocks)

    def second_layer(cot):
        probs = probs_of()
        return (probs,) + backward(query_rows, kk, vv, probs, cot)

    def first_layer_probs(cot):
        return (probs_of(),) + zeros()

    probs, dq_first, band_first, far_first = lax.cond(
        section_one, second_layer, first_layer_probs, out_grad
    )
    sent_back = dq_first.astype(jnp.bfloat16)
    arrived = from_behind(sent_back, "section", -1)
    dq_second, band_second, far_second = lax.cond(
        section_one,
        lambda cot: zeros(),
        lambda cot: backward(query_rows, kk, vv, probs, cot),
        arrived,
    )
    band_grad = jnp.where(section_one, band_first, band_second)
    far = jnp.where(section_one, far_first, far_second)
    total = gather_grads(far, anchor_pick.reshape(-1), nanch, rows_per_slot)
    owner = (anchor_blocks[rank] == blocks).astype(jnp.float32)
    owned = owner[:, None, None] * total[None]
    kv_grad = (band_grad + owned.reshape(band_grad.shape)).astype(jnp.bfloat16)
    input_grad = jnp.where(section_one, sent_back, dq_second.astype(jnp.bfloat16))
    return (input_grad[None], kv_grad[None])


def solution(mesh):
    ny = 8
    devs = mesh.devices
    grid = Mesh(
        devs.reshape(devs.shape[0], devs.shape[1] // ny, ny, devs.shape[2]),
        ("section", "cx", "cy", "head"),
    )
    ctx = ("cx", "cy")
    placed = (
        P("section", ctx, "head"),
        P("section", ctx, "head"),
        P(ctx, "head"),
        P(ctx),
        P(),
        P(ctx, None),
    )
    return jax.shard_map(
        body,
        mesh=grid,
        in_specs=placed,
        out_specs=(P("section", ctx, "head"), P("section", ctx, "head")),
        check_vma=False,
    )
```

```python
import jax
import jax.numpy as jnp
from jax import lax
from jax.sharding import Mesh, PartitionSpec as P

HEAD_SIZE = 128
BLK = 128


def from_behind(x, axis, by):
    peers = lax.axis_size(axis)
    pairs = [(i, i + by) for i in range(peers) if 0 <= i + by < peers]
    return lax.ppermute(x, axis, pairs)


def gather_keys(keyvals, anchor_kv, picks):
    rows, feat = keyvals.shape
    kvh = feat // (2 * HEAD_SIZE)
    per_dev = rows // BLK
    npick = picks.shape[1]
    nanch = anchor_kv.shape[0]
    own = keyvals.reshape(per_dev, BLK, kvh, 2, HEAD_SIZE)
    far = anchor_kv.reshape(nanch, BLK, kvh, 2, HEAD_SIZE)[picks].reshape(
        per_dev, npick * BLK, kvh, 2, HEAD_SIZE
    )
    keys = jnp.concatenate([own, far], axis=1)
    return keys[:, :, :, 0], keys[:, :, :, 1]


def forward(query_rows, kk, sentences, picks, anchor_blocks, blocks):
    rows, width = query_rows.shape
    kvh = kk.shape[2]
    group_size = width // (kvh * HEAD_SIZE)
    per_dev = rows // BLK
    npick = picks.shape[1]
    scale = HEAD_SIZE ** (-0.5)
    q_blocks = query_rows.reshape(per_dev, BLK, kvh, group_size, HEAD_SIZE)
    score = (
        jnp.einsum("bqkgd,blkd->bkgql", q_blocks, kk, preferred_element_type=jnp.float32) * scale
    )
    sent = sentences.reshape(per_dev, BLK)
    idx = jnp.arange(BLK, dtype=jnp.int32)
    band = (idx[None, :, None] >= idx[None, None, :]) & (sent[:, :, None] == sent[:, None, :])
    valid = jnp.repeat(anchor_blocks[picks] < blocks[:, None], BLK, axis=1)
    far_mask = jnp.broadcast_to(valid[:, None, :], (per_dev, BLK, npick * BLK))
    mask = jnp.concatenate([band, far_mask], axis=2)[:, None, None]
    score = jnp.where(mask, score, jnp.float32(-1e30))
    top = jnp.max(score, axis=-1, keepdims=True)
    expo = jnp.exp(score - top)
    return expo / jnp.sum(expo, axis=-1, keepdims=True)


def backward(query_rows, kk, vv, probs, cot):
    rows, width = query_rows.shape
    kvh = kk.shape[2]
    feat = 2 * kvh * HEAD_SIZE
    group_size = width // (kvh * HEAD_SIZE)
    per_dev = rows // BLK
    scale = HEAD_SIZE ** (-0.5)
    q_blocks = query_rows.reshape(per_dev, BLK, kvh, group_size, HEAD_SIZE)
    pb = probs.astype(jnp.bfloat16)
    outp = jnp.einsum("bkgql,blkd->bqkgd", pb, vv, preferred_element_type=jnp.float32)
    c_blocks = cot.reshape(per_dev, BLK, kvh, group_size, HEAD_SIZE)
    delta = jnp.sum(c_blocks.astype(jnp.float32) * outp, axis=-1).transpose(0, 2, 3, 1)[..., None]
    dprob = jnp.einsum("bqkgd,blkd->bkgql", c_blocks, vv, preferred_element_type=jnp.float32)
    dscore = (probs * (dprob - delta)).astype(jnp.bfloat16)
    dq = jnp.einsum("bkgql,blkd->bqkgd", dscore, kk, preferred_element_type=jnp.float32) * scale
    dk = (
        jnp.einsum("bkgql,bqkgd->blkd", dscore, q_blocks, preferred_element_type=jnp.float32)
        * scale
    )
    dv = jnp.einsum("bkgql,bqkgd->blkd", pb, c_blocks, preferred_element_type=jnp.float32)
    dkv = jnp.stack([dk, dv], axis=3)
    band_grad = dkv[:, :BLK].reshape(rows, feat)
    far_grad = dkv[:, BLK:].reshape(-1, BLK, feat)
    return (dq.reshape(rows, width), band_grad, far_grad)


def spread_anchors(mine, rows_per_slot):
    ny = lax.axis_size("cy")
    nx = lax.axis_size("cx")
    blk, feat = mine.shape
    part = mine.reshape(ny, blk // ny, feat)
    got = lax.all_to_all(part, "cy", 0, 0, tiled=True)
    row = jnp.sum(got.astype(jnp.float32), axis=0).astype(mine.dtype)
    got = lax.all_to_all(jnp.broadcast_to(row[None], (nx,) + row.shape), "cx", 0, 0, tiled=True)
    nslot = nx // rows_per_slot
    slots = jnp.sum(
        got.reshape(nslot, rows_per_slot, *row.shape).astype(jnp.float32), axis=1
    ).astype(mine.dtype)
    got = lax.all_to_all(jnp.broadcast_to(slots[None], (ny,) + slots.shape), "cy", 0, 0, tiled=True)
    return got.transpose(1, 0, 2, 3).reshape(nslot, blk, feat)


def gather_grads(far, picks, nslot, rows_per_slot):
    ny = lax.axis_size("cy")
    npick, blk, feat = far.shape
    size = (blk // ny) * feat
    data = far.reshape(npick, ny, size)
    tag = jnp.broadcast_to(picks.astype(jnp.float32)[:, None, None], (npick, ny, 128))
    load = jnp.concatenate([data, tag], axis=2).transpose(1, 0, 2)
    got = lax.all_to_all(load, "cy", 0, 0, tiled=True)
    vals = got[:, :, :size]
    ids = got[:, :, size]
    slot_ids = jnp.arange(nslot, dtype=jnp.float32)
    rowsum = jnp.sum(
        jnp.where(ids[None, :, :, None] == slot_ids[:, None, None, None], vals[None], 0.0),
        axis=(1, 2),
    ).reshape(nslot, blk // ny, feat)
    got = lax.all_to_all(jnp.repeat(rowsum, rows_per_slot, axis=0), "cx", 0, 0, tiled=True)
    total = jnp.sum(got, axis=0)
    got = lax.all_to_all(jnp.broadcast_to(total[None], (ny,) + total.shape), "cy", 0, 0, tiled=True)
    return got.reshape(blk, feat)


def body(layer_in, kv_in, out_grad, sentences, anchor_blocks, anchor_pick):
    query_rows = layer_in[0]
    keyvals = kv_in[0]
    rows, width = query_rows.shape
    feat = keyvals.shape[1]
    per_dev = rows // BLK
    nanch = anchor_blocks.shape[0]
    rows_per_slot = lax.axis_size("cx") // nanch
    ctx = lax.axis_index("cx") * lax.axis_size("cy") + lax.axis_index("cy")
    rank = lax.axis_index("cx") // rows_per_slot
    section_one = lax.axis_index("section") == 1
    blocks = ctx * per_dev + jnp.arange(per_dev, dtype=jnp.int32)
    kv_blocks = keyvals.reshape(per_dev, BLK, feat)
    hit = anchor_blocks[None, :] == blocks[:, None]
    holder = jnp.any(hit, axis=1)[:, None, None]
    mine = jnp.where(holder, kv_blocks, jnp.zeros_like(kv_blocks)).sum(axis=0, dtype=jnp.float32)
    mine = mine.astype(jnp.bfloat16)
    anchor_kv = spread_anchors(mine, rows_per_slot)
    npick = anchor_pick.shape[1]
    kk, vv = gather_keys(keyvals, anchor_kv, anchor_pick)

    probs = forward(query_rows, kk, sentences, anchor_pick, anchor_blocks, blocks)

    sent_back = lax.cond(
        section_one,
        lambda cot: backward(query_rows, kk, vv, probs, cot)[0].astype(jnp.bfloat16),
        lambda cot: cot,
        out_grad,
    )
    arrived = from_behind(sent_back, "section", -1)
    cot = jnp.where(section_one, out_grad, arrived)
    dq, band_grad, far = backward(query_rows, kk, vv, probs, cot)
    total = gather_grads(far, anchor_pick.reshape(-1), nanch, rows_per_slot)
    owner = (anchor_blocks[rank] == blocks).astype(jnp.float32)
    owned = owner[:, None, None] * total[None]
    kv_grad = (band_grad + owned.reshape(band_grad.shape)).astype(jnp.bfloat16)
    input_grad = jnp.where(section_one, sent_back, dq.astype(jnp.bfloat16))
    return (input_grad[None], kv_grad[None])


def solution(mesh):
    ny = 8
    devs = mesh.devices
    grid = Mesh(
        devs.reshape(devs.shape[0], devs.shape[1] // ny, ny, devs.shape[2]),
        ("section", "cx", "cy", "head"),
    )
    ctx = ("cx", "cy")
    placed = (
        P("section", ctx, "head"),
        P("section", ctx, "head"),
        P(ctx, "head"),
        P(ctx),
        P(),
        P(ctx, None),
    )
    return jax.shard_map(
        body,
        mesh=grid,
        in_specs=placed,
        out_specs=(P("section", ctx, "head"), P("section", ctx, "head")),
        check_vma=False,
    )
```

```python
import jax
import jax.numpy as jnp
from jax import lax
from jax.sharding import Mesh, PartitionSpec as P

HEAD_SIZE = 128
BLK = 128


def from_behind(x, axis, by):
    peers = lax.axis_size(axis)
    pairs = [(i, i + by) for i in range(peers) if 0 <= i + by < peers]
    return lax.ppermute(x, axis, pairs)


def gather_keys(keyvals, anchor_kv, picks):
    rows, feat = keyvals.shape
    kvh = feat // (2 * HEAD_SIZE)
    per_dev = rows // BLK
    npick = picks.shape[1]
    nanch = anchor_kv.shape[0]
    own = keyvals.reshape(per_dev, BLK, kvh, 2, HEAD_SIZE)
    far = anchor_kv.reshape(nanch, BLK, kvh, 2, HEAD_SIZE)[picks].reshape(
        per_dev, npick * BLK, kvh, 2, HEAD_SIZE
    )
    keys = jnp.concatenate([own, far], axis=1)
    return keys[:, :, :, 0], keys[:, :, :, 1]


def forward(query_rows, kk, sentences, picks, anchor_blocks, blocks):
    rows, width = query_rows.shape
    kvh = kk.shape[2]
    group_size = width // (kvh * HEAD_SIZE)
    per_dev = rows // BLK
    npick = picks.shape[1]
    scale = HEAD_SIZE ** (-0.5)
    q_blocks = query_rows.reshape(per_dev, BLK, kvh, group_size, HEAD_SIZE)
    score = (
        jnp.einsum("bqkgd,blkd->bkgql", q_blocks, kk, preferred_element_type=jnp.float32) * scale
    )
    sent = sentences.reshape(per_dev, BLK)
    idx = jnp.arange(BLK, dtype=jnp.int32)
    band = (idx[None, :, None] >= idx[None, None, :]) & (sent[:, :, None] == sent[:, None, :])
    valid = jnp.repeat(anchor_blocks[picks] < blocks[:, None], BLK, axis=1)
    far_mask = jnp.broadcast_to(valid[:, None, :], (per_dev, BLK, npick * BLK))
    mask = jnp.concatenate([band, far_mask], axis=2)[:, None, None]
    score = jnp.where(mask, score, jnp.float32(-1e30))
    top = jnp.max(score, axis=-1, keepdims=True)
    expo = jnp.exp(score - top)
    return expo / jnp.sum(expo, axis=-1, keepdims=True)


def backward(query_rows, kk, vv, probs, cot):
    rows, width = query_rows.shape
    kvh = kk.shape[2]
    feat = 2 * kvh * HEAD_SIZE
    group_size = width // (kvh * HEAD_SIZE)
    per_dev = rows // BLK
    scale = HEAD_SIZE ** (-0.5)
    q_blocks = query_rows.reshape(per_dev, BLK, kvh, group_size, HEAD_SIZE)
    pb = probs.astype(jnp.bfloat16)
    outp = jnp.einsum("bkgql,blkd->bqkgd", pb, vv, preferred_element_type=jnp.float32)
    c_blocks = cot.reshape(per_dev, BLK, kvh, group_size, HEAD_SIZE)
    delta = jnp.sum(c_blocks.astype(jnp.float32) * outp, axis=-1).transpose(0, 2, 3, 1)[..., None]
    dprob = jnp.einsum("bqkgd,blkd->bkgql", c_blocks, vv, preferred_element_type=jnp.float32)
    dscore = (probs * (dprob - delta)).astype(jnp.bfloat16)
    dq = jnp.einsum("bkgql,blkd->bqkgd", dscore, kk, preferred_element_type=jnp.float32) * scale
    dk = (
        jnp.einsum("bkgql,bqkgd->blkd", dscore, q_blocks, preferred_element_type=jnp.float32)
        * scale
    )
    dv = jnp.einsum("bkgql,bqkgd->blkd", pb, c_blocks, preferred_element_type=jnp.float32)
    dkv = jnp.stack([dk, dv], axis=3)
    band_grad = dkv[:, :BLK].reshape(rows, feat)
    far_grad = dkv[:, BLK:].reshape(-1, BLK, feat)
    return (dq.reshape(rows, width), band_grad, far_grad)


def spread_anchors(mine, rows_per_slot):
    ny = lax.axis_size("cy")
    nx = lax.axis_size("cx")
    blk, feat = mine.shape
    part = mine.reshape(ny, blk // ny, feat)
    got = lax.all_to_all(part, "cy", 0, 0, tiled=True)
    row = jnp.sum(got.astype(jnp.float32), axis=0).astype(mine.dtype)
    got = lax.all_to_all(jnp.broadcast_to(row[None], (nx,) + row.shape), "cx", 0, 0, tiled=True)
    nslot = nx // rows_per_slot
    slots = jnp.sum(
        got.reshape(nslot, rows_per_slot, *row.shape).astype(jnp.float32), axis=1
    ).astype(mine.dtype)
    got = lax.all_to_all(jnp.broadcast_to(slots[None], (ny,) + slots.shape), "cy", 0, 0, tiled=True)
    return got.transpose(1, 0, 2, 3).reshape(nslot, blk, feat)


def gather_grads(far, picks, nslot, rows_per_slot):
    ny = lax.axis_size("cy")
    npick, blk, feat = far.shape
    size = (blk // ny) * feat
    data = far.reshape(npick, ny, size)
    tag = jnp.broadcast_to(picks.astype(jnp.float32)[:, None, None], (npick, ny, 128))
    load = jnp.concatenate([data, tag], axis=2).transpose(1, 0, 2)
    got = lax.all_to_all(load, "cy", 0, 0, tiled=True)
    vals = got[:, :, :size]
    ids = got[:, :, size]
    slot_ids = jnp.arange(nslot, dtype=jnp.float32)
    rowsum = jnp.sum(
        jnp.where(ids[None, :, :, None] == slot_ids[:, None, None, None], vals[None], 0.0),
        axis=(1, 2),
    ).reshape(nslot, blk // ny, feat)
    got = lax.all_to_all(jnp.repeat(rowsum, rows_per_slot, axis=0), "cx", 0, 0, tiled=True)
    total = jnp.sum(got, axis=0)
    got = lax.all_to_all(jnp.broadcast_to(total[None], (ny,) + total.shape), "cy", 0, 0, tiled=True)
    return got.reshape(blk, feat)


def body(layer_in, kv_in, out_grad, sentences, anchor_blocks, anchor_pick):
    query_rows = layer_in[0]
    keyvals = kv_in[0]
    rows, width = query_rows.shape
    feat = keyvals.shape[1]
    per_dev = rows // BLK
    nanch = anchor_blocks.shape[0]
    rows_per_slot = lax.axis_size("cx") // nanch
    ctx = lax.axis_index("cx") * lax.axis_size("cy") + lax.axis_index("cy")
    rank = lax.axis_index("cx") // rows_per_slot
    section_one = lax.axis_index("section") == 1
    blocks = ctx * per_dev + jnp.arange(per_dev, dtype=jnp.int32)
    kv_blocks = keyvals.reshape(per_dev, BLK, feat)
    hit = anchor_blocks[None, :] == blocks[:, None]
    holder = jnp.any(hit, axis=1)[:, None, None]
    mine = jnp.where(holder, kv_blocks, jnp.zeros_like(kv_blocks)).sum(axis=0, dtype=jnp.float32)
    mine = mine.astype(jnp.bfloat16)
    anchor_kv = spread_anchors(mine, rows_per_slot)
    npick = anchor_pick.shape[1]
    kk, vv = gather_keys(keyvals, anchor_kv, anchor_pick)

    def probs_of():
        return forward(query_rows, kk, sentences, anchor_pick, anchor_blocks, blocks)

    def relayed(probs, cot):
        dq, band, far = backward(query_rows, kk, vv, probs, cot)
        return dq.astype(jnp.bfloat16), band, far

    def second_layer(cot):
        probs = probs_of()
        return (probs,) + relayed(probs, cot)

    def first_layer_probs(cot):
        return (
            probs_of(),
            cot,
            jnp.zeros((rows, feat), jnp.float32),
            jnp.zeros((per_dev * npick, BLK, feat), jnp.float32),
        )

    probs, sent_back, band_first, far_first = lax.cond(
        section_one, second_layer, first_layer_probs, out_grad
    )
    arrived = from_behind(sent_back, "section", -1)
    dq_out, band_grad, far = lax.cond(
        section_one,
        lambda cot: (sent_back, band_first, far_first),
        lambda cot: relayed(probs, cot),
        arrived,
    )
    total = gather_grads(far, anchor_pick.reshape(-1), nanch, rows_per_slot)
    owner = (anchor_blocks[rank] == blocks).astype(jnp.float32)
    owned = owner[:, None, None] * total[None]
    kv_grad = (band_grad + owned.reshape(band_grad.shape)).astype(jnp.bfloat16)
    input_grad = dq_out
    return (input_grad[None], kv_grad[None])


def solution(mesh):
    ny = 8
    devs = mesh.devices
    grid = Mesh(
        devs.reshape(devs.shape[0], devs.shape[1] // ny, ny, devs.shape[2]),
        ("section", "cx", "cy", "head"),
    )
    ctx = ("cx", "cy")
    placed = (
        P("section", ctx, "head"),
        P("section", ctx, "head"),
        P(ctx, "head"),
        P(ctx),
        P(),
        P(ctx, None),
    )
    return jax.shard_map(
        body,
        mesh=grid,
        in_specs=placed,
        out_specs=(P("section", ctx, "head"), P("section", ctx, "head")),
        check_vma=False,
    )
```

```python
import jax
import jax.numpy as jnp
from jax import lax
from jax.sharding import Mesh, PartitionSpec as P

HEAD_SIZE = 128
BLK = 128


def from_behind(x, axis, by):
    peers = lax.axis_size(axis)
    pairs = [(i, i + by) for i in range(peers) if 0 <= i + by < peers]
    return lax.ppermute(x, axis, pairs)


def gather_keys(keyvals, anchor_kv, picks):
    rows, feat = keyvals.shape
    kvh = feat // (2 * HEAD_SIZE)
    per_dev = rows // BLK
    npick = picks.shape[1]
    nanch = anchor_kv.shape[0]
    own = keyvals.reshape(per_dev, BLK, kvh, 2, HEAD_SIZE)
    far = anchor_kv.reshape(nanch, BLK, kvh, 2, HEAD_SIZE)[picks].reshape(
        per_dev, npick * BLK, kvh, 2, HEAD_SIZE
    )
    keys = jnp.concatenate([own, far], axis=1)
    return keys[:, :, :, 0], keys[:, :, :, 1]


def forward(query_rows, kk, sentences, picks, anchor_blocks, blocks):
    rows, width = query_rows.shape
    kvh = kk.shape[2]
    group_size = width // (kvh * HEAD_SIZE)
    per_dev = rows // BLK
    npick = picks.shape[1]
    scale = HEAD_SIZE ** (-0.5)
    q_blocks = query_rows.reshape(per_dev, BLK, kvh, group_size, HEAD_SIZE)
    score = (
        jnp.einsum("bqkgd,blkd->bkgql", q_blocks, kk, preferred_element_type=jnp.float32) * scale
    )
    sent = sentences.reshape(per_dev, BLK)
    idx = jnp.arange(BLK, dtype=jnp.int32)
    band = (idx[None, :, None] >= idx[None, None, :]) & (sent[:, :, None] == sent[:, None, :])
    valid = jnp.repeat(anchor_blocks[picks] < blocks[:, None], BLK, axis=1)
    far_mask = jnp.broadcast_to(valid[:, None, :], (per_dev, BLK, npick * BLK))
    mask = jnp.concatenate([band, far_mask], axis=2)[:, None, None]
    score = jnp.where(mask, score, jnp.float32(-1e30))
    top = jnp.max(score, axis=-1, keepdims=True)
    expo = jnp.exp(score - top)
    return expo / jnp.sum(expo, axis=-1, keepdims=True)


def backward(query_rows, kk, vv, probs, cot):
    rows, width = query_rows.shape
    kvh = kk.shape[2]
    feat = 2 * kvh * HEAD_SIZE
    group_size = width // (kvh * HEAD_SIZE)
    per_dev = rows // BLK
    scale = HEAD_SIZE ** (-0.5)
    q_blocks = query_rows.reshape(per_dev, BLK, kvh, group_size, HEAD_SIZE)
    pb = probs.astype(jnp.bfloat16)
    outp = jnp.einsum("bkgql,blkd->bqkgd", pb, vv, preferred_element_type=jnp.float32)
    c_blocks = cot.reshape(per_dev, BLK, kvh, group_size, HEAD_SIZE)
    delta = jnp.sum(c_blocks.astype(jnp.float32) * outp, axis=-1).transpose(0, 2, 3, 1)[..., None]
    dprob = jnp.einsum("bqkgd,blkd->bkgql", c_blocks, vv, preferred_element_type=jnp.float32)
    dscore = (probs * (dprob - delta)).astype(jnp.bfloat16)
    dq = jnp.einsum("bkgql,blkd->bqkgd", dscore, kk, preferred_element_type=jnp.float32) * scale
    dk = (
        jnp.einsum("bkgql,bqkgd->blkd", dscore, q_blocks, preferred_element_type=jnp.float32)
        * scale
    )
    dv = jnp.einsum("bkgql,bqkgd->blkd", pb, c_blocks, preferred_element_type=jnp.float32)
    dkv = jnp.stack([dk, dv], axis=3)
    band_grad = dkv[:, :BLK].reshape(rows, feat)
    far_grad = dkv[:, BLK:].reshape(-1, BLK, feat)
    return (dq.reshape(rows, width), band_grad, far_grad)


def spread_anchors(mine, rows_per_slot):
    ny = lax.axis_size("cy")
    nx = lax.axis_size("cx")
    blk, feat = mine.shape
    part = mine.reshape(ny, blk // ny, feat)
    got = lax.all_to_all(part, "cy", 0, 0, tiled=True)
    row = jnp.sum(got.astype(jnp.float32), axis=0).astype(mine.dtype)
    got = lax.all_to_all(jnp.broadcast_to(row[None], (nx,) + row.shape), "cx", 0, 0, tiled=True)
    nslot = nx // rows_per_slot
    slots = jnp.sum(
        got.reshape(nslot, rows_per_slot, *row.shape).astype(jnp.float32), axis=1
    ).astype(mine.dtype)
    got = lax.all_to_all(jnp.broadcast_to(slots[None], (ny,) + slots.shape), "cy", 0, 0, tiled=True)
    return got.transpose(1, 0, 2, 3).reshape(nslot, blk, feat)


def gather_grads(far, picks, nslot, rows_per_slot):
    ny = lax.axis_size("cy")
    npick, blk, feat = far.shape
    size = (blk // ny) * feat
    data = far.reshape(npick, ny, size)
    tag = jnp.broadcast_to(picks.astype(jnp.float32)[:, None, None], (npick, ny, 128))
    load = jnp.concatenate([data, tag], axis=2).transpose(1, 0, 2)
    got = lax.all_to_all(load, "cy", 0, 0, tiled=True)
    vals = got[:, :, :size]
    ids = got[:, :, size]
    slot_ids = jnp.arange(nslot, dtype=jnp.float32)
    rowsum = jnp.sum(
        jnp.where(ids[None, :, :, None] == slot_ids[:, None, None, None], vals[None], 0.0),
        axis=(1, 2),
    ).reshape(nslot, blk // ny, feat)
    got = lax.all_to_all(jnp.repeat(rowsum, rows_per_slot, axis=0), "cx", 0, 0, tiled=True)
    total = jnp.sum(got, axis=0)
    got = lax.all_to_all(jnp.broadcast_to(total[None], (ny,) + total.shape), "cy", 0, 0, tiled=True)
    return got.reshape(blk, feat)


def body(layer_in, kv_in, out_grad, sentences, anchor_blocks, anchor_pick):
    query_rows = layer_in[0]
    keyvals = kv_in[0]
    rows, width = query_rows.shape
    feat = keyvals.shape[1]
    per_dev = rows // BLK
    nanch = anchor_blocks.shape[0]
    rows_per_slot = lax.axis_size("cx") // nanch
    ctx = lax.axis_index("cx") * lax.axis_size("cy") + lax.axis_index("cy")
    rank = lax.axis_index("cx") // rows_per_slot
    section_one = lax.axis_index("section") == 1
    blocks = ctx * per_dev + jnp.arange(per_dev, dtype=jnp.int32)
    kv_blocks = keyvals.reshape(per_dev, BLK, feat)
    holder = (anchor_blocks[rank] == blocks)[:, None, None]
    mine = jnp.where(holder, kv_blocks, jnp.zeros_like(kv_blocks)).sum(axis=0, dtype=jnp.float32)
    mine = mine.astype(jnp.bfloat16)
    anchor_kv = spread_anchors(mine, rows_per_slot)
    npick = anchor_pick.shape[1]
    kk, vv = gather_keys(keyvals, anchor_kv, anchor_pick)

    def probs_of():
        return forward(query_rows, kk, sentences, anchor_pick, anchor_blocks, blocks)

    def relayed(probs, cot):
        dq, band, far = backward(query_rows, kk, vv, probs, cot)
        return dq.astype(jnp.bfloat16), band, far

    def second_layer(cot):
        probs = probs_of()
        return (probs,) + relayed(probs, cot)

    def first_layer_probs(cot):
        return (
            probs_of(),
            cot,
            jnp.zeros((rows, feat), jnp.float32),
            jnp.zeros((per_dev * npick, BLK, feat), jnp.float32),
        )

    probs, sent_back, band_first, far_first = lax.cond(
        section_one, second_layer, first_layer_probs, out_grad
    )
    arrived = from_behind(sent_back, "section", -1)
    dq_out, band_grad, far = lax.cond(
        section_one,
        lambda cot: (sent_back, band_first, far_first),
        lambda cot: relayed(probs, cot),
        arrived,
    )
    total = gather_grads(far, anchor_pick.reshape(-1), nanch, rows_per_slot)
    owner = (anchor_blocks[rank] == blocks).astype(jnp.float32)
    owned = owner[:, None, None] * total[None]
    kv_grad = (band_grad + owned.reshape(band_grad.shape)).astype(jnp.bfloat16)
    input_grad = dq_out
    return (input_grad[None], kv_grad[None])


def solution(mesh):
    ny = 8
    devs = mesh.devices
    grid = Mesh(
        devs.reshape(devs.shape[0], devs.shape[1] // ny, ny, devs.shape[2]),
        ("section", "cx", "cy", "head"),
    )
    ctx = ("cx", "cy")
    placed = (
        P("section", ctx, "head"),
        P("section", ctx, "head"),
        P(ctx, "head"),
        P(ctx),
        P(),
        P(ctx, None),
    )
    return jax.shard_map(
        body,
        mesh=grid,
        in_specs=placed,
        out_specs=(P("section", ctx, "head"), P("section", ctx, "head")),
        check_vma=False,
    )
```

```python
import jax
import jax.numpy as jnp
from jax import lax
from jax.sharding import Mesh, PartitionSpec as P

HEAD_SIZE = 128
BLK = 128


def from_behind(x, axis, by):
    peers = lax.axis_size(axis)
    pairs = [(i, i + by) for i in range(peers) if 0 <= i + by < peers]
    return lax.ppermute(x, axis, pairs)


def gather_keys(keyvals, anchor_kv, picks):
    rows, feat = keyvals.shape
    kvh = feat // (2 * HEAD_SIZE)
    per_dev = rows // BLK
    npick = picks.shape[1]
    nanch = anchor_kv.shape[0]
    own = keyvals.reshape(per_dev, BLK, kvh, 2, HEAD_SIZE)
    far = anchor_kv.reshape(nanch, BLK, kvh, 2, HEAD_SIZE)[picks].reshape(
        per_dev, npick * BLK, kvh, 2, HEAD_SIZE
    )
    keys = jnp.concatenate([own, far], axis=1)
    return keys[:, :, :, 0], keys[:, :, :, 1]


def forward(query_rows, kk, sentences, picks, anchor_blocks, blocks):
    rows, width = query_rows.shape
    assert rows == BLK and kk.shape[0] == 1 and kk.shape[2] == 1
    group_size = width // HEAD_SIZE
    npick = picks.shape[1]
    scale = HEAD_SIZE ** (-0.5)
    q2 = query_rows.reshape(rows * group_size, HEAD_SIZE)
    keys = kk.reshape(-1, HEAD_SIZE)
    score = lax.dot_general(
        q2, keys, (((1,), (1,)), ((), ())), preferred_element_type=jnp.float32
    ) * scale
    sent = sentences.reshape(BLK)
    idx = jnp.arange(BLK, dtype=jnp.int32)
    band = (idx[:, None] >= idx[None, :]) & (sent[:, None] == sent[None, :])
    valid = jnp.repeat(anchor_blocks[picks[0]] < blocks[0], BLK)
    mask = jnp.concatenate([band, jnp.broadcast_to(valid[None, :], (BLK, npick * BLK))], axis=1)
    mask = jnp.broadcast_to(mask[:, None, :], (BLK, group_size, mask.shape[1]))
    score = jnp.where(mask.reshape(score.shape), score, jnp.float32(-1e30))
    top = jnp.max(score, axis=-1, keepdims=True)
    expo = jnp.exp(score - top)
    return expo / jnp.sum(expo, axis=-1, keepdims=True)


def backward(query_rows, kk, vv, probs, cot):
    rows, width = query_rows.shape
    feat = 2 * HEAD_SIZE
    scale = HEAD_SIZE ** (-0.5)
    q2 = query_rows.reshape(-1, HEAD_SIZE)
    c2 = cot.reshape(-1, HEAD_SIZE)
    keys = kk.reshape(-1, HEAD_SIZE)
    vals = vv.reshape(-1, HEAD_SIZE)
    f32 = jnp.float32
    pb = probs.astype(jnp.bfloat16)
    outp = lax.dot_general(pb, vals, (((1,), (0,)), ((), ())), preferred_element_type=f32)
    delta = jnp.sum(c2.astype(f32) * outp, axis=-1, keepdims=True)
    dprob = lax.dot_general(c2, vals, (((1,), (1,)), ((), ())), preferred_element_type=f32)
    dscore = (probs * (dprob - delta)).astype(jnp.bfloat16)
    dq = lax.dot_general(dscore, keys, (((1,), (0,)), ((), ())), preferred_element_type=f32) * scale
    dk = lax.dot_general(dscore, q2, (((0,), (0,)), ((), ())), preferred_element_type=f32) * scale
    dv = lax.dot_general(pb, c2, (((0,), (0,)), ((), ())), preferred_element_type=f32)
    dkv = jnp.stack([dk, dv], axis=1).reshape(-1, feat)
    band_grad = dkv[:BLK]
    far_grad = dkv[BLK:].reshape(-1, BLK, feat)
    return (dq.reshape(rows, width), band_grad, far_grad)


def spread_anchors(mine, rows_per_slot):
    ny = lax.axis_size("cy")
    nx = lax.axis_size("cx")
    blk, feat = mine.shape
    part = mine.reshape(ny, blk // ny, feat)
    got = lax.all_to_all(part, "cy", 0, 0, tiled=True)
    row = jnp.sum(got.astype(jnp.float32), axis=0).astype(mine.dtype)
    got = lax.all_to_all(jnp.broadcast_to(row[None], (nx,) + row.shape), "cx", 0, 0, tiled=True)
    nslot = nx // rows_per_slot
    slots = jnp.sum(
        got.reshape(nslot, rows_per_slot, *row.shape).astype(jnp.float32), axis=1
    ).astype(mine.dtype)
    got = lax.all_to_all(jnp.broadcast_to(slots[None], (ny,) + slots.shape), "cy", 0, 0, tiled=True)
    return got.transpose(1, 0, 2, 3).reshape(nslot, blk, feat)


def gather_grads(far, picks, nslot, rows_per_slot):
    ny = lax.axis_size("cy")
    npick, blk, feat = far.shape
    size = (blk // ny) * feat
    data = far.reshape(npick, ny, size)
    tag = jnp.broadcast_to(picks.astype(jnp.float32)[:, None, None], (npick, ny, 128))
    load = jnp.concatenate([data, tag], axis=2).transpose(1, 0, 2)
    got = lax.all_to_all(load, "cy", 0, 0, tiled=True)
    vals = got[:, :, :size]
    ids = got[:, :, size]
    slot_ids = jnp.arange(nslot, dtype=jnp.float32)
    rowsum = jnp.sum(
        jnp.where(ids[None, :, :, None] == slot_ids[:, None, None, None], vals[None], 0.0),
        axis=(1, 2),
    ).reshape(nslot, blk // ny, feat)
    got = lax.all_to_all(jnp.repeat(rowsum, rows_per_slot, axis=0), "cx", 0, 0, tiled=True)
    total = jnp.sum(got, axis=0)
    got = lax.all_to_all(jnp.broadcast_to(total[None], (ny,) + total.shape), "cy", 0, 0, tiled=True)
    return got.reshape(blk, feat)


def body(layer_in, kv_in, out_grad, sentences, anchor_blocks, anchor_pick):
    query_rows = layer_in[0]
    keyvals = kv_in[0]
    rows, width = query_rows.shape
    feat = keyvals.shape[1]
    per_dev = rows // BLK
    nanch = anchor_blocks.shape[0]
    rows_per_slot = lax.axis_size("cx") // nanch
    ctx = lax.axis_index("cx") * lax.axis_size("cy") + lax.axis_index("cy")
    rank = lax.axis_index("cx") // rows_per_slot
    section_one = lax.axis_index("section") == 1
    blocks = ctx * per_dev + jnp.arange(per_dev, dtype=jnp.int32)
    kv_blocks = keyvals.reshape(per_dev, BLK, feat)
    holder = (anchor_blocks[rank] == blocks)[:, None, None]
    mine = jnp.where(holder, kv_blocks, jnp.zeros_like(kv_blocks)).sum(axis=0, dtype=jnp.float32)
    mine = mine.astype(jnp.bfloat16)
    anchor_kv = spread_anchors(mine, rows_per_slot)
    npick = anchor_pick.shape[1]
    kk, vv = gather_keys(keyvals, anchor_kv, anchor_pick)

    def probs_of():
        return forward(query_rows, kk, sentences, anchor_pick, anchor_blocks, blocks)

    def relayed(probs, cot):
        dq, band, far = backward(query_rows, kk, vv, probs, cot)
        return dq.astype(jnp.bfloat16), band, far

    def second_layer(cot):
        probs = probs_of()
        return (probs,) + relayed(probs, cot)

    def first_layer_probs(cot):
        return (
            probs_of(),
            cot,
            jnp.zeros((rows, feat), jnp.float32),
            jnp.zeros((per_dev * npick, BLK, feat), jnp.float32),
        )

    probs, sent_back, band_first, far_first = lax.cond(
        section_one, second_layer, first_layer_probs, out_grad
    )
    arrived = from_behind(sent_back, "section", -1)
    dq_out, band_grad, far = lax.cond(
        section_one,
        lambda cot: (sent_back, band_first, far_first),
        lambda cot: relayed(probs, cot),
        arrived,
    )
    total = gather_grads(far, anchor_pick.reshape(-1), nanch, rows_per_slot)
    owner = (anchor_blocks[rank] == blocks).astype(jnp.float32)
    owned = owner[:, None, None] * total[None]
    kv_grad = (band_grad + owned.reshape(band_grad.shape)).astype(jnp.bfloat16)
    input_grad = dq_out
    return (input_grad[None], kv_grad[None])


def solution(mesh):
    ny = 8
    devs = mesh.devices
    grid = Mesh(
        devs.reshape(devs.shape[0], devs.shape[1] // ny, ny, devs.shape[2]),
        ("section", "cx", "cy", "head"),
    )
    ctx = ("cx", "cy")
    placed = (
        P("section", ctx, "head"),
        P("section", ctx, "head"),
        P(ctx, "head"),
        P(ctx),
        P(),
        P(ctx, None),
    )
    return jax.shard_map(
        body,
        mesh=grid,
        in_specs=placed,
        out_specs=(P("section", ctx, "head"), P("section", ctx, "head")),
        check_vma=False,
    )
```

```python
import jax
import jax.numpy as jnp
from jax import lax
from jax.sharding import Mesh, PartitionSpec as P

HEAD_SIZE = 128
BLK = 128


def from_behind(x, axis, by):
    peers = lax.axis_size(axis)
    pairs = [(i, i + by) for i in range(peers) if 0 <= i + by < peers]
    return lax.ppermute(x, axis, pairs)


def gather_keys(keyvals, anchor_kv, picks):
    rows, feat = keyvals.shape
    kvh = feat // (2 * HEAD_SIZE)
    per_dev = rows // BLK
    npick = picks.shape[1]
    nanch = anchor_kv.shape[0]
    own = keyvals.reshape(per_dev, BLK, kvh, 2, HEAD_SIZE)
    far = anchor_kv.reshape(nanch, BLK, kvh, 2, HEAD_SIZE)[picks].reshape(
        per_dev, npick * BLK, kvh, 2, HEAD_SIZE
    )
    keys = jnp.concatenate([own, far], axis=1)
    return keys[:, :, :, 0], keys[:, :, :, 1]


def forward(query_rows, kk, sentences, picks, anchor_blocks, blocks):
    rows, width = query_rows.shape
    kvh = kk.shape[2]
    group_size = width // (kvh * HEAD_SIZE)
    per_dev = rows // BLK
    npick = picks.shape[1]
    scale = HEAD_SIZE ** (-0.5)
    q_blocks = query_rows.reshape(per_dev, BLK, kvh, group_size, HEAD_SIZE)
    score = (
        jnp.einsum("bqkgd,blkd->bkgql", q_blocks, kk, preferred_element_type=jnp.float32) * scale
    )
    sent = sentences.reshape(per_dev, BLK)
    idx = jnp.arange(BLK, dtype=jnp.int32)
    band = (idx[None, :, None] >= idx[None, None, :]) & (sent[:, :, None] == sent[:, None, :])
    valid = jnp.repeat(anchor_blocks[picks] < blocks[:, None], BLK, axis=1)
    far_mask = jnp.broadcast_to(valid[:, None, :], (per_dev, BLK, npick * BLK))
    mask = jnp.concatenate([band, far_mask], axis=2)[:, None, None]
    score = jnp.where(mask, score, jnp.float32(-1e30))
    top = jnp.max(score, axis=-1, keepdims=True)
    expo = jnp.exp(score - top)
    return expo / jnp.sum(expo, axis=-1, keepdims=True)


def backward(query_rows, kk, vv, probs, cot):
    rows, width = query_rows.shape
    kvh = kk.shape[2]
    feat = 2 * kvh * HEAD_SIZE
    group_size = width // (kvh * HEAD_SIZE)
    per_dev = rows // BLK
    scale = HEAD_SIZE ** (-0.5)
    q_blocks = query_rows.reshape(per_dev, BLK, kvh, group_size, HEAD_SIZE)
    pb = probs.astype(jnp.bfloat16)
    outp = jnp.einsum("bkgql,blkd->bqkgd", pb, vv, preferred_element_type=jnp.float32)
    c_blocks = cot.reshape(per_dev, BLK, kvh, group_size, HEAD_SIZE)
    delta = jnp.sum(c_blocks.astype(jnp.float32) * outp, axis=-1).transpose(0, 2, 3, 1)[..., None]
    dprob = jnp.einsum("bqkgd,blkd->bkgql", c_blocks, vv, preferred_element_type=jnp.float32)
    dscore = (probs * (dprob - delta)).astype(jnp.bfloat16)
    dq = jnp.einsum("bkgql,blkd->bqkgd", dscore, kk, preferred_element_type=jnp.float32) * scale
    dk = (
        jnp.einsum("bkgql,bqkgd->blkd", dscore, q_blocks, preferred_element_type=jnp.float32)
        * scale
    )
    dv = jnp.einsum("bkgql,bqkgd->blkd", pb, c_blocks, preferred_element_type=jnp.float32)
    dkv = jnp.stack([dk, dv], axis=3)
    band_grad = dkv[:, :BLK].reshape(rows, feat)
    far_grad = dkv[:, BLK:].reshape(-1, BLK, feat)
    return (dq.reshape(rows, width), band_grad, far_grad)


def spread_anchors(mine, rows_per_slot):
    ny = lax.axis_size("cy")
    nx = lax.axis_size("cx")
    blk, feat = mine.shape
    got = lax.all_to_all(jnp.broadcast_to(mine[None], (ny, blk, feat)), "cy", 0, 0, tiled=True)
    row = jnp.sum(got.astype(jnp.float32), axis=0).astype(mine.dtype)
    got = lax.all_to_all(jnp.broadcast_to(row[None], (nx, blk, feat)), "cx", 0, 0, tiled=True)
    nslot = nx // rows_per_slot
    return jnp.sum(
        got.reshape(nslot, rows_per_slot, blk, feat).astype(jnp.float32), axis=1
    ).astype(mine.dtype)


def gather_grads(far, picks, nslot, rows_per_slot):
    ny = lax.axis_size("cy")
    npick, blk, feat = far.shape
    size = (blk // ny) * feat
    data = far.reshape(npick, ny, size)
    tag = jnp.broadcast_to(picks.astype(jnp.float32)[:, None, None], (npick, ny, 128))
    load = jnp.concatenate([data, tag], axis=2).transpose(1, 0, 2)
    got = lax.all_to_all(load, "cy", 0, 0, tiled=True)
    vals = got[:, :, :size]
    ids = got[:, :, size]
    slot_ids = jnp.arange(nslot, dtype=jnp.float32)
    rowsum = jnp.sum(
        jnp.where(ids[None, :, :, None] == slot_ids[:, None, None, None], vals[None], 0.0),
        axis=(1, 2),
    ).reshape(nslot, blk // ny, feat)
    got = lax.all_to_all(jnp.repeat(rowsum, rows_per_slot, axis=0), "cx", 0, 0, tiled=True)
    total = jnp.sum(got, axis=0)
    got = lax.all_to_all(jnp.broadcast_to(total[None], (ny,) + total.shape), "cy", 0, 0, tiled=True)
    return got.reshape(blk, feat)


def body(layer_in, kv_in, out_grad, sentences, anchor_blocks, anchor_pick):
    query_rows = layer_in[0]
    keyvals = kv_in[0]
    rows, width = query_rows.shape
    feat = keyvals.shape[1]
    per_dev = rows // BLK
    nanch = anchor_blocks.shape[0]
    rows_per_slot = lax.axis_size("cx") // nanch
    ctx = lax.axis_index("cx") * lax.axis_size("cy") + lax.axis_index("cy")
    rank = lax.axis_index("cx") // rows_per_slot
    section_one = lax.axis_index("section") == 1
    blocks = ctx * per_dev + jnp.arange(per_dev, dtype=jnp.int32)
    kv_blocks = keyvals.reshape(per_dev, BLK, feat)
    holder = (anchor_blocks[rank] == blocks)[:, None, None]
    mine = jnp.where(holder, kv_blocks, jnp.zeros_like(kv_blocks)).sum(axis=0, dtype=jnp.float32)
    mine = mine.astype(jnp.bfloat16)
    anchor_kv = spread_anchors(mine, rows_per_slot)
    npick = anchor_pick.shape[1]
    kk, vv = gather_keys(keyvals, anchor_kv, anchor_pick)

    def probs_of():
        return forward(query_rows, kk, sentences, anchor_pick, anchor_blocks, blocks)

    def relayed(probs, cot):
        dq, band, far = backward(query_rows, kk, vv, probs, cot)
        return dq.astype(jnp.bfloat16), band, far

    def second_layer(cot):
        probs = probs_of()
        return (probs,) + relayed(probs, cot)

    def first_layer_probs(cot):
        return (
            probs_of(),
            cot,
            jnp.zeros((rows, feat), jnp.float32),
            jnp.zeros((per_dev * npick, BLK, feat), jnp.float32),
        )

    probs, sent_back, band_first, far_first = lax.cond(
        section_one, second_layer, first_layer_probs, out_grad
    )
    arrived = from_behind(sent_back, "section", -1)
    dq_out, band_grad, far = lax.cond(
        section_one,
        lambda cot: (sent_back, band_first, far_first),
        lambda cot: relayed(probs, cot),
        arrived,
    )
    total = gather_grads(far, anchor_pick.reshape(-1), nanch, rows_per_slot)
    owner = (anchor_blocks[rank] == blocks).astype(jnp.float32)
    owned = owner[:, None, None] * total[None]
    kv_grad = (band_grad + owned.reshape(band_grad.shape)).astype(jnp.bfloat16)
    input_grad = dq_out
    return (input_grad[None], kv_grad[None])


def solution(mesh):
    ny = 8
    devs = mesh.devices
    grid = Mesh(
        devs.reshape(devs.shape[0], devs.shape[1] // ny, ny, devs.shape[2]),
        ("section", "cx", "cy", "head"),
    )
    ctx = ("cx", "cy")
    placed = (
        P("section", ctx, "head"),
        P("section", ctx, "head"),
        P(ctx, "head"),
        P(ctx),
        P(),
        P(ctx, None),
    )
    return jax.shard_map(
        body,
        mesh=grid,
        in_specs=placed,
        out_specs=(P("section", ctx, "head"), P("section", ctx, "head")),
        check_vma=False,
    )
```

```python
import jax
import jax.numpy as jnp
from jax import lax
from jax.experimental import pallas as pl
from jax.experimental.pallas import tpu as pltpu
from jax.sharding import Mesh, PartitionSpec as P

HEAD_SIZE = 128
BLK = 128


def from_behind(x, axis, by):
    peers = lax.axis_size(axis)
    pairs = [(i, i + by) for i in range(peers) if 0 <= i + by < peers]
    return lax.ppermute(x, axis, pairs)


def gather_keys(keyvals, anchor_kv, picks):
    rows, feat = keyvals.shape
    kvh = feat // (2 * HEAD_SIZE)
    per_dev = rows // BLK
    npick = picks.shape[1]
    nanch = anchor_kv.shape[0]
    own = keyvals.reshape(per_dev, BLK, kvh, 2, HEAD_SIZE)
    far = anchor_kv.reshape(nanch, BLK, kvh, 2, HEAD_SIZE)[picks].reshape(
        per_dev, npick * BLK, kvh, 2, HEAD_SIZE
    )
    keys = jnp.concatenate([own, far], axis=1)
    return keys[:, :, :, 0], keys[:, :, :, 1]


def attn_kernel(q_ref, k_ref, v_ref, c_ref, m_ref, dq_ref, dk_ref, dv_ref):
    f32 = jnp.float32
    scale = HEAD_SIZE ** (-0.5)
    keys = k_ref[...]
    vals = v_ref[...]
    keep = m_ref[...] > 0.5
    nt = (((1,), (1,)), ((), ()))
    nn = (((1,), (0,)), ((), ()))
    tn = (((0,), (0,)), ((), ()))
    dk = jnp.zeros(dk_ref.shape, f32)
    dv = jnp.zeros(dv_ref.shape, f32)
    for g in range(q_ref.shape[1] // HEAD_SIZE):
        cols = slice(g * HEAD_SIZE, (g + 1) * HEAD_SIZE)
        qg = q_ref[:, cols]
        cg = c_ref[:, cols]
        score = lax.dot_general(qg, keys, nt, preferred_element_type=f32) * scale
        score = jnp.where(keep, score, f32(-1e30))
        top = jnp.max(score, axis=-1, keepdims=True)
        expo = jnp.exp(score - top)
        probs = expo / jnp.sum(expo, axis=-1, keepdims=True)
        pb = probs.astype(jnp.bfloat16)
        outp = lax.dot_general(pb, vals, nn, preferred_element_type=f32)
        delta = jnp.sum(cg.astype(f32) * outp, axis=-1, keepdims=True)
        dprob = lax.dot_general(cg, vals, nt, preferred_element_type=f32)
        dscore = (probs * (dprob - delta)).astype(jnp.bfloat16)
        dq_ref[:, cols] = lax.dot_general(dscore, keys, nn, preferred_element_type=f32) * scale
        dk = dk + lax.dot_general(dscore, qg, tn, preferred_element_type=f32)
        dv = dv + lax.dot_general(pb, cg, tn, preferred_element_type=f32)
    dk_ref[...] = dk * scale
    dv_ref[...] = dv


def attend(query_rows, kk, vv, mask, cot):
    rows, width = query_rows.shape
    nkeys = kk.shape[0]
    vmem = pl.BlockSpec(memory_space=pltpu.VMEM)
    dq, dk, dv = pl.pallas_call(
        attn_kernel,
        out_shape=(
            jax.ShapeDtypeStruct((rows, width), jnp.float32),
            jax.ShapeDtypeStruct((nkeys, HEAD_SIZE), jnp.float32),
            jax.ShapeDtypeStruct((nkeys, HEAD_SIZE), jnp.float32),
        ),
        in_specs=[vmem] * 5,
        out_specs=(vmem, vmem, vmem),
    )(query_rows, kk, vv, cot, mask)
    dkv = jnp.stack([dk, dv], axis=1).reshape(nkeys, 2 * HEAD_SIZE)
    return dq, dkv[:BLK], dkv[BLK:].reshape(-1, BLK, 2 * HEAD_SIZE)


def mask_of(sentences, picks, anchor_blocks, blocks):
    npick = picks.shape[1]
    sent = sentences.reshape(BLK)
    idx = jnp.arange(BLK, dtype=jnp.int32)
    band = (idx[:, None] >= idx[None, :]) & (sent[:, None] == sent[None, :])
    valid = jnp.repeat(anchor_blocks[picks[0]] < blocks[0], BLK)
    mask = jnp.concatenate([band, jnp.broadcast_to(valid[None, :], (BLK, npick * BLK))], axis=1)
    return mask.astype(jnp.float32)


def spread_anchors(mine, rows_per_slot):
    ny = lax.axis_size("cy")
    nx = lax.axis_size("cx")
    blk, feat = mine.shape
    part = mine.reshape(ny, blk // ny, feat)
    got = lax.all_to_all(part, "cy", 0, 0, tiled=True)
    row = jnp.sum(got.astype(jnp.float32), axis=0).astype(mine.dtype)
    got = lax.all_to_all(jnp.broadcast_to(row[None], (nx,) + row.shape), "cx", 0, 0, tiled=True)
    nslot = nx // rows_per_slot
    slots = jnp.sum(
        got.reshape(nslot, rows_per_slot, *row.shape).astype(jnp.float32), axis=1
    ).astype(mine.dtype)
    got = lax.all_to_all(jnp.broadcast_to(slots[None], (ny,) + slots.shape), "cy", 0, 0, tiled=True)
    return got.transpose(1, 0, 2, 3).reshape(nslot, blk, feat)


def gather_grads(far, picks, nslot, rows_per_slot):
    ny = lax.axis_size("cy")
    npick, blk, feat = far.shape
    size = (blk // ny) * feat
    data = far.reshape(npick, ny, size)
    tag = jnp.broadcast_to(picks.astype(jnp.float32)[:, None, None], (npick, ny, 128))
    load = jnp.concatenate([data, tag], axis=2).transpose(1, 0, 2)
    got = lax.all_to_all(load, "cy", 0, 0, tiled=True)
    vals = got[:, :, :size]
    ids = got[:, :, size]
    slot_ids = jnp.arange(nslot, dtype=jnp.float32)
    rowsum = jnp.sum(
        jnp.where(ids[None, :, :, None] == slot_ids[:, None, None, None], vals[None], 0.0),
        axis=(1, 2),
    ).reshape(nslot, blk // ny, feat)
    got = lax.all_to_all(jnp.repeat(rowsum, rows_per_slot, axis=0), "cx", 0, 0, tiled=True)
    total = jnp.sum(got, axis=0)
    got = lax.all_to_all(jnp.broadcast_to(total[None], (ny,) + total.shape), "cy", 0, 0, tiled=True)
    return got.reshape(blk, feat)


def body(layer_in, kv_in, out_grad, sentences, anchor_blocks, anchor_pick):
    query_rows = layer_in[0]
    keyvals = kv_in[0]
    rows, width = query_rows.shape
    feat = keyvals.shape[1]
    per_dev = rows // BLK
    nanch = anchor_blocks.shape[0]
    rows_per_slot = lax.axis_size("cx") // nanch
    ctx = lax.axis_index("cx") * lax.axis_size("cy") + lax.axis_index("cy")
    rank = lax.axis_index("cx") // rows_per_slot
    section_one = lax.axis_index("section") == 1
    blocks = ctx * per_dev + jnp.arange(per_dev, dtype=jnp.int32)
    kv_blocks = keyvals.reshape(per_dev, BLK, feat)
    hit = anchor_blocks[None, :] == blocks[:, None]
    holder = jnp.any(hit, axis=1)[:, None, None]
    mine = jnp.where(holder, kv_blocks, jnp.zeros_like(kv_blocks)).sum(axis=0, dtype=jnp.float32)
    mine = mine.astype(jnp.bfloat16)
    anchor_kv = spread_anchors(mine, rows_per_slot)
    npick = anchor_pick.shape[1]
    kk, vv = gather_keys(keyvals, anchor_kv, anchor_pick)

    assert per_dev == 1 and feat == 2 * HEAD_SIZE
    keys = kk.reshape(-1, HEAD_SIZE)
    vals = vv.reshape(-1, HEAD_SIZE)
    mask = mask_of(sentences, anchor_pick, anchor_blocks, blocks)

    def relayed(cot):
        dq, band, far = attend(query_rows, keys, vals, mask, cot)
        return dq.astype(jnp.bfloat16), band, far

    def waiting(cot):
        return (
            cot,
            jnp.zeros((rows, feat), jnp.float32),
            jnp.zeros((per_dev * npick, BLK, feat), jnp.float32),
        )

    sent_back, band_first, far_first = lax.cond(section_one, relayed, waiting, out_grad)
    arrived = from_behind(sent_back, "section", -1)
    dq_out, band_grad, far = lax.cond(
        section_one,
        lambda cot: (sent_back, band_first, far_first),
        relayed,
        arrived,
    )
    total = gather_grads(far, anchor_pick.reshape(-1), nanch, rows_per_slot)
    owner = (anchor_blocks[rank] == blocks).astype(jnp.float32)
    owned = owner[:, None, None] * total[None]
    kv_grad = (band_grad + owned.reshape(band_grad.shape)).astype(jnp.bfloat16)
    input_grad = dq_out
    return (input_grad[None], kv_grad[None])


def solution(mesh):
    ny = 8
    devs = mesh.devices
    grid = Mesh(
        devs.reshape(devs.shape[0], devs.shape[1] // ny, ny, devs.shape[2]),
        ("section", "cx", "cy", "head"),
    )
    ctx = ("cx", "cy")
    placed = (
        P("section", ctx, "head"),
        P("section", ctx, "head"),
        P(ctx, "head"),
        P(ctx),
        P(),
        P(ctx, None),
    )
    return jax.shard_map(
        body,
        mesh=grid,
        in_specs=placed,
        out_specs=(P("section", ctx, "head"), P("section", ctx, "head")),
        check_vma=False,
    )
```

```python
import jax
import jax.numpy as jnp
from jax import lax
from jax.sharding import Mesh, PartitionSpec as P

HEAD_SIZE = 128
BLK = 128


def from_behind(x, axis, by):
    peers = lax.axis_size(axis)
    pairs = [(i, i + by) for i in range(peers) if 0 <= i + by < peers]
    return lax.ppermute(x, axis, pairs)


def gather_keys(keyvals, anchor_kv, picks):
    rows, feat = keyvals.shape
    kvh = feat // (2 * HEAD_SIZE)
    per_dev = rows // BLK
    npick = picks.shape[1]
    nanch = anchor_kv.shape[0]
    own = keyvals.reshape(per_dev, BLK, kvh, 2, HEAD_SIZE)
    far = anchor_kv.reshape(nanch, BLK, kvh, 2, HEAD_SIZE)[picks].reshape(
        per_dev, npick * BLK, kvh, 2, HEAD_SIZE
    )
    keys = jnp.concatenate([own, far], axis=1)
    return keys[:, :, :, 0], keys[:, :, :, 1]


def forward(query_rows, kk, sentences, picks, anchor_blocks, blocks):
    rows, width = query_rows.shape
    kvh = kk.shape[2]
    group_size = width // (kvh * HEAD_SIZE)
    per_dev = rows // BLK
    npick = picks.shape[1]
    scale = HEAD_SIZE ** (-0.5)
    q_blocks = query_rows.reshape(per_dev, BLK, kvh, group_size, HEAD_SIZE)
    score = (
        jnp.einsum("bqkgd,blkd->bkgql", q_blocks, kk, preferred_element_type=jnp.float32) * scale
    )
    sent = sentences.reshape(per_dev, BLK)
    idx = jnp.arange(BLK, dtype=jnp.int32)
    band = (idx[None, :, None] >= idx[None, None, :]) & (sent[:, :, None] == sent[:, None, :])
    valid = jnp.repeat(anchor_blocks[picks] < blocks[:, None], BLK, axis=1)
    far_mask = jnp.broadcast_to(valid[:, None, :], (per_dev, BLK, npick * BLK))
    mask = jnp.concatenate([band, far_mask], axis=2)[:, None, None]
    score = jnp.where(mask, score, jnp.float32(-1e30))
    top = jnp.max(score, axis=-1, keepdims=True)
    expo = jnp.exp(score - top)
    return expo / jnp.sum(expo, axis=-1, keepdims=True)


def backward(query_rows, kk, vv, probs, cot):
    dscore, pb = scores_grad(kk, vv, probs, cot)
    dq, band_grad = near_grads(query_rows, kk, cot, dscore, pb)
    return (dq, band_grad, far_grads(query_rows, cot, dscore, pb))


def scores_grad(kk, vv, probs, cot):
    per_dev, nkeys, kvh, _ = kk.shape
    width = cot.shape[1]
    group_size = width // (kvh * HEAD_SIZE)
    pb = probs.astype(jnp.bfloat16)
    outp = jnp.einsum("bkgql,blkd->bqkgd", pb, vv, preferred_element_type=jnp.float32)
    c_blocks = cot.reshape(per_dev, BLK, kvh, group_size, HEAD_SIZE)
    delta = jnp.sum(c_blocks.astype(jnp.float32) * outp, axis=-1).transpose(0, 2, 3, 1)[..., None]
    dprob = jnp.einsum("bqkgd,blkd->bkgql", c_blocks, vv, preferred_element_type=jnp.float32)
    dscore = (probs * (dprob - delta)).astype(jnp.bfloat16)
    return dscore, pb


def key_grads(query_rows, cot, dscore, pb, cols):
    rows, width = query_rows.shape
    per_dev, kvh, group_size = dscore.shape[:3]
    scale = HEAD_SIZE ** (-0.5)
    q_blocks = query_rows.reshape(per_dev, BLK, kvh, group_size, HEAD_SIZE)
    c_blocks = cot.reshape(per_dev, BLK, kvh, group_size, HEAD_SIZE)
    ds = dscore[..., cols]
    p = pb[..., cols]
    dk = jnp.einsum("bkgql,bqkgd->blkd", ds, q_blocks, preferred_element_type=jnp.float32) * scale
    dv = jnp.einsum("bkgql,bqkgd->blkd", p, c_blocks, preferred_element_type=jnp.float32)
    return jnp.stack([dk, dv], axis=3)


def far_grads(query_rows, cot, dscore, pb):
    feat = 2 * dscore.shape[1] * HEAD_SIZE
    dkv = key_grads(query_rows, cot, dscore, pb, slice(BLK, None))
    return dkv.reshape(-1, BLK, feat)


def near_grads(query_rows, kk, cot, dscore, pb):
    rows, width = query_rows.shape
    feat = 2 * dscore.shape[1] * HEAD_SIZE
    scale = HEAD_SIZE ** (-0.5)
    dq = jnp.einsum("bkgql,blkd->bqkgd", dscore, kk, preferred_element_type=jnp.float32) * scale
    band_grad = key_grads(query_rows, cot, dscore, pb, slice(0, BLK)).reshape(rows, feat)
    return dq.reshape(rows, width), band_grad


def spread_anchors(mine, rows_per_slot):
    ny = lax.axis_size("cy")
    nx = lax.axis_size("cx")
    blk, feat = mine.shape
    part = mine.reshape(ny, blk // ny, feat)
    got = lax.all_to_all(part, "cy", 0, 0, tiled=True)
    row = jnp.sum(got.astype(jnp.float32), axis=0).astype(mine.dtype)
    got = lax.all_to_all(jnp.broadcast_to(row[None], (nx,) + row.shape), "cx", 0, 0, tiled=True)
    nslot = nx // rows_per_slot
    slots = jnp.sum(
        got.reshape(nslot, rows_per_slot, *row.shape).astype(jnp.float32), axis=1
    ).astype(mine.dtype)
    got = lax.all_to_all(jnp.broadcast_to(slots[None], (ny,) + slots.shape), "cy", 0, 0, tiled=True)
    return got.transpose(1, 0, 2, 3).reshape(nslot, blk, feat)


def gather_grads(far, picks, nslot, rows_per_slot):
    ny = lax.axis_size("cy")
    npick, blk, feat = far.shape
    size = (blk // ny) * feat
    data = far.reshape(npick, ny, size)
    tag = jnp.broadcast_to(picks.astype(jnp.float32)[:, None, None], (npick, ny, 128))
    load = jnp.concatenate([data, tag], axis=2).transpose(1, 0, 2)
    got = lax.all_to_all(load, "cy", 0, 0, tiled=True)
    vals = got[:, :, :size]
    ids = got[:, :, size]
    slot_ids = jnp.arange(nslot, dtype=jnp.float32)
    rowsum = jnp.sum(
        jnp.where(ids[None, :, :, None] == slot_ids[:, None, None, None], vals[None], 0.0),
        axis=(1, 2),
    ).reshape(nslot, blk // ny, feat)
    got = lax.all_to_all(jnp.repeat(rowsum, rows_per_slot, axis=0), "cx", 0, 0, tiled=True)
    total = jnp.sum(got, axis=0)
    got = lax.all_to_all(jnp.broadcast_to(total[None], (ny,) + total.shape), "cy", 0, 0, tiled=True)
    return got.reshape(blk, feat)


def body(layer_in, kv_in, out_grad, sentences, anchor_blocks, anchor_pick):
    query_rows = layer_in[0]
    keyvals = kv_in[0]
    rows, width = query_rows.shape
    feat = keyvals.shape[1]
    per_dev = rows // BLK
    nanch = anchor_blocks.shape[0]
    rows_per_slot = lax.axis_size("cx") // nanch
    ctx = lax.axis_index("cx") * lax.axis_size("cy") + lax.axis_index("cy")
    rank = lax.axis_index("cx") // rows_per_slot
    section_one = lax.axis_index("section") == 1
    blocks = ctx * per_dev + jnp.arange(per_dev, dtype=jnp.int32)
    kv_blocks = keyvals.reshape(per_dev, BLK, feat)
    hit = anchor_blocks[None, :] == blocks[:, None]
    holder = jnp.any(hit, axis=1)[:, None, None]
    mine = jnp.where(holder, kv_blocks, jnp.zeros_like(kv_blocks)).sum(axis=0, dtype=jnp.float32)
    mine = mine.astype(jnp.bfloat16)
    anchor_kv = spread_anchors(mine, rows_per_slot)
    npick = anchor_pick.shape[1]
    kk, vv = gather_keys(keyvals, anchor_kv, anchor_pick)

    def probs_of():
        return forward(query_rows, kk, sentences, anchor_pick, anchor_blocks, blocks)

    def relayed(probs, cot):
        dq, band, far = backward(query_rows, kk, vv, probs, cot)
        return dq.astype(jnp.bfloat16), band, far

    def second_layer(cot):
        probs = probs_of()
        return (probs,) + relayed(probs, cot)

    def first_layer_probs(cot):
        return (
            probs_of(),
            cot,
            jnp.zeros((rows, feat), jnp.float32),
            jnp.zeros((per_dev * npick, BLK, feat), jnp.float32),
        )

    probs, sent_back, band_first, far_first = lax.cond(
        section_one, second_layer, first_layer_probs, out_grad
    )
    arrived = from_behind(sent_back, "section", -1)
    far, dscore, pb = lax.cond(
        section_one,
        lambda cot: (far_first, jnp.zeros_like(probs, jnp.bfloat16), jnp.zeros_like(probs, jnp.bfloat16)),
        lambda cot: (lambda ds, p: (far_grads(query_rows, cot, ds, p), ds, p))(
            *scores_grad(kk, vv, probs, cot)
        ),
        arrived,
    )
    total = gather_grads(far, anchor_pick.reshape(-1), nanch, rows_per_slot)
    dq_out, band_grad = lax.cond(
        section_one,
        lambda cot: (sent_back, band_first),
        lambda cot: (lambda dq, band: (dq.astype(jnp.bfloat16), band))(
            *near_grads(query_rows, kk, cot, dscore, pb)
        ),
        arrived,
    )
    owner = (anchor_blocks[rank] == blocks).astype(jnp.float32)
    owned = owner[:, None, None] * total[None]
    kv_grad = (band_grad + owned.reshape(band_grad.shape)).astype(jnp.bfloat16)
    input_grad = dq_out
    return (input_grad[None], kv_grad[None])


def solution(mesh):
    ny = 8
    devs = mesh.devices
    grid = Mesh(
        devs.reshape(devs.shape[0], devs.shape[1] // ny, ny, devs.shape[2]),
        ("section", "cx", "cy", "head"),
    )
    ctx = ("cx", "cy")
    placed = (
        P("section", ctx, "head"),
        P("section", ctx, "head"),
        P(ctx, "head"),
        P(ctx),
        P(),
        P(ctx, None),
    )
    return jax.shard_map(
        body,
        mesh=grid,
        in_specs=placed,
        out_specs=(P("section", ctx, "head"), P("section", ctx, "head")),
        check_vma=False,
    )
```

```python
import jax
import jax.numpy as jnp
from jax import lax
from jax.sharding import Mesh, PartitionSpec as P

HEAD_SIZE = 128
BLK = 128


def from_behind(x, axis, by):
    peers = lax.axis_size(axis)
    pairs = [(i, i + by) for i in range(peers) if 0 <= i + by < peers]
    return lax.ppermute(x, axis, pairs)


def gather_keys(keyvals, anchor_kv, picks):
    rows, feat = keyvals.shape
    kvh = feat // (2 * HEAD_SIZE)
    per_dev = rows // BLK
    npick = picks.shape[1]
    nanch = anchor_kv.shape[0]
    own = keyvals.reshape(per_dev, BLK, kvh, 2, HEAD_SIZE)
    far = anchor_kv.reshape(nanch, BLK, kvh, 2, HEAD_SIZE)[picks].reshape(
        per_dev, npick * BLK, kvh, 2, HEAD_SIZE
    )
    keys = jnp.concatenate([own, far], axis=1)
    return keys[:, :, :, 0], keys[:, :, :, 1]


def forward(query_rows, kk, sentences, picks, anchor_blocks, blocks):
    rows, width = query_rows.shape
    kvh = kk.shape[2]
    group_size = width // (kvh * HEAD_SIZE)
    per_dev = rows // BLK
    npick = picks.shape[1]
    scale = HEAD_SIZE ** (-0.5)
    q_blocks = query_rows.reshape(per_dev, BLK, kvh, group_size, HEAD_SIZE)
    score = (
        jnp.einsum("bqkgd,blkd->bkgql", q_blocks, kk, preferred_element_type=jnp.float32) * scale
    )
    sent = sentences.reshape(per_dev, BLK)
    idx = jnp.arange(BLK, dtype=jnp.int32)
    band = (idx[None, :, None] >= idx[None, None, :]) & (sent[:, :, None] == sent[:, None, :])
    valid = jnp.repeat(anchor_blocks[picks] < blocks[:, None], BLK, axis=1)
    far_mask = jnp.broadcast_to(valid[:, None, :], (per_dev, BLK, npick * BLK))
    mask = jnp.concatenate([band, far_mask], axis=2)[:, None, None]
    score = jnp.where(mask, score, jnp.float32(-1e30))
    top = jnp.max(score, axis=-1, keepdims=True)
    expo = jnp.exp(score - top)
    return expo / jnp.sum(expo, axis=-1, keepdims=True)


def backward(query_rows, kk, vv, probs, cot):
    rows, width = query_rows.shape
    kvh = kk.shape[2]
    feat = 2 * kvh * HEAD_SIZE
    group_size = width // (kvh * HEAD_SIZE)
    per_dev = rows // BLK
    scale = HEAD_SIZE ** (-0.5)
    q_blocks = query_rows.reshape(per_dev, BLK, kvh, group_size, HEAD_SIZE)
    pb = probs.astype(jnp.bfloat16)
    outp = jnp.einsum("bkgql,blkd->bqkgd", pb, vv, preferred_element_type=jnp.float32)
    c_blocks = cot.reshape(per_dev, BLK, kvh, group_size, HEAD_SIZE)
    delta = jnp.sum(c_blocks.astype(jnp.float32) * outp, axis=-1).transpose(0, 2, 3, 1)[..., None]
    dprob = jnp.einsum("bqkgd,blkd->bkgql", c_blocks, vv, preferred_element_type=jnp.float32)
    dscore = (probs * (dprob - delta)).astype(jnp.bfloat16)
    dq = jnp.einsum("bkgql,blkd->bqkgd", dscore, kk, preferred_element_type=jnp.float32) * scale
    dk = (
        jnp.einsum("bkgql,bqkgd->blkd", dscore, q_blocks, preferred_element_type=jnp.float32)
        * scale
    )
    dv = jnp.einsum("bkgql,bqkgd->blkd", pb, c_blocks, preferred_element_type=jnp.float32)
    dkv = jnp.stack([dk, dv], axis=3)
    band_grad = dkv[:, :BLK].reshape(rows, feat)
    far_grad = dkv[:, BLK:].reshape(-1, BLK, feat)
    return (dq.reshape(rows, width), band_grad, far_grad)


def spread_anchors(mine, rows_per_slot):
    ny = lax.axis_size("cy")
    nx = lax.axis_size("cx")
    blk, feat = mine.shape
    part = mine.reshape(ny, blk // ny, feat)
    got = lax.all_to_all(part, "cy", 0, 0, tiled=True)
    row = jnp.sum(got.astype(jnp.float32), axis=0).astype(mine.dtype)
    got = lax.all_to_all(jnp.broadcast_to(row[None], (nx,) + row.shape), "cx", 0, 0, tiled=True)
    nslot = nx // rows_per_slot
    slots = jnp.sum(
        got.reshape(nslot, rows_per_slot, *row.shape).astype(jnp.float32), axis=1
    ).astype(mine.dtype)
    got = lax.all_to_all(jnp.broadcast_to(slots[None], (ny,) + slots.shape), "cy", 0, 0, tiled=True)
    return got.transpose(1, 0, 2, 3).reshape(nslot, blk, feat)


def gather_grads(far, picks, nslot, rows_per_slot):
    ny = lax.axis_size("cy")
    npick, blk, feat = far.shape
    size = (blk // ny) * feat
    data = far.reshape(npick, ny, size)
    tag = jnp.broadcast_to(picks.astype(jnp.float32)[:, None, None], (npick, ny, 128))
    load = jnp.concatenate([data, tag], axis=2).transpose(1, 0, 2)
    got = lax.all_to_all(load, "cy", 0, 0, tiled=True)
    vals = got[:, :, :size]
    ids = got[:, :, size]
    slot_ids = jnp.arange(nslot, dtype=jnp.float32)
    rowsum = jnp.sum(
        jnp.where(ids[None, :, :, None] == slot_ids[:, None, None, None], vals[None], 0.0),
        axis=(1, 2),
    ).reshape(nslot, blk // ny, feat)
    part = jnp.repeat(rowsum.astype(jnp.bfloat16), rows_per_slot, axis=0)
    got = lax.all_to_all(part, "cx", 0, 0, tiled=True)
    total = jnp.sum(got.astype(jnp.float32), axis=0).astype(jnp.bfloat16)
    got = lax.all_to_all(jnp.broadcast_to(total[None], (ny,) + total.shape), "cy", 0, 0, tiled=True)
    return got.reshape(blk, feat).astype(jnp.float32)


def body(layer_in, kv_in, out_grad, sentences, anchor_blocks, anchor_pick):
    query_rows = layer_in[0]
    keyvals = kv_in[0]
    rows, width = query_rows.shape
    feat = keyvals.shape[1]
    per_dev = rows // BLK
    nanch = anchor_blocks.shape[0]
    rows_per_slot = lax.axis_size("cx") // nanch
    ctx = lax.axis_index("cx") * lax.axis_size("cy") + lax.axis_index("cy")
    rank = lax.axis_index("cx") // rows_per_slot
    section_one = lax.axis_index("section") == 1
    blocks = ctx * per_dev + jnp.arange(per_dev, dtype=jnp.int32)
    kv_blocks = keyvals.reshape(per_dev, BLK, feat)
    hit = anchor_blocks[None, :] == blocks[:, None]
    holder = jnp.any(hit, axis=1)[:, None, None]
    mine = jnp.where(holder, kv_blocks, jnp.zeros_like(kv_blocks)).sum(axis=0, dtype=jnp.float32)
    mine = mine.astype(jnp.bfloat16)
    anchor_kv = spread_anchors(mine, rows_per_slot)
    npick = anchor_pick.shape[1]
    kk, vv = gather_keys(keyvals, anchor_kv, anchor_pick)

    def probs_of():
        return forward(query_rows, kk, sentences, anchor_pick, anchor_blocks, blocks)

    def relayed(probs, cot):
        dq, band, far = backward(query_rows, kk, vv, probs, cot)
        return dq.astype(jnp.bfloat16), band, far

    def second_layer(cot):
        probs = probs_of()
        return (probs,) + relayed(probs, cot)

    def first_layer_probs(cot):
        return (
            probs_of(),
            cot,
            jnp.zeros((rows, feat), jnp.float32),
            jnp.zeros((per_dev * npick, BLK, feat), jnp.float32),
        )

    probs, sent_back, band_first, far_first = lax.cond(
        section_one, second_layer, first_layer_probs, out_grad
    )
    arrived = from_behind(sent_back, "section", -1)
    dq_out, band_grad, far = lax.cond(
        section_one,
        lambda cot: (sent_back, band_first, far_first),
        lambda cot: relayed(probs, cot),
        arrived,
    )
    total = gather_grads(far, anchor_pick.reshape(-1), nanch, rows_per_slot)
    owner = (anchor_blocks[rank] == blocks).astype(jnp.float32)
    owned = owner[:, None, None] * total[None]
    kv_grad = (band_grad + owned.reshape(band_grad.shape)).astype(jnp.bfloat16)
    input_grad = dq_out
    return (input_grad[None], kv_grad[None])


def solution(mesh):
    ny = 8
    devs = mesh.devices
    grid = Mesh(
        devs.reshape(devs.shape[0], devs.shape[1] // ny, ny, devs.shape[2]),
        ("section", "cx", "cy", "head"),
    )
    ctx = ("cx", "cy")
    placed = (
        P("section", ctx, "head"),
        P("section", ctx, "head"),
        P(ctx, "head"),
        P(ctx),
        P(),
        P(ctx, None),
    )
    return jax.shard_map(
        body,
        mesh=grid,
        in_specs=placed,
        out_specs=(P("section", ctx, "head"), P("section", ctx, "head")),
        check_vma=False,
    )
```

```python
import jax
import jax.numpy as jnp
from jax import lax
from jax.sharding import Mesh, PartitionSpec as P

HEAD_SIZE = 128
BLK = 128


def from_behind(x, axis, by):
    peers = lax.axis_size(axis)
    pairs = [(i, i + by) for i in range(peers) if 0 <= i + by < peers]
    return lax.ppermute(x, axis, pairs)


def gather_keys(keyvals, anchor_kv, picks):
    rows, feat = keyvals.shape
    kvh = feat // (2 * HEAD_SIZE)
    per_dev = rows // BLK
    npick = picks.shape[1]
    nanch = anchor_kv.shape[0]
    own = keyvals.reshape(per_dev, BLK, kvh, 2, HEAD_SIZE)
    far = anchor_kv.reshape(nanch, BLK, kvh, 2, HEAD_SIZE)[picks].reshape(
        per_dev, npick * BLK, kvh, 2, HEAD_SIZE
    )
    keys = jnp.concatenate([own, far], axis=1)
    return keys[:, :, :, 0], keys[:, :, :, 1]


def forward(query_rows, kk, sentences, picks, anchor_blocks, blocks):
    rows, width = query_rows.shape
    kvh = kk.shape[2]
    group_size = width // (kvh * HEAD_SIZE)
    per_dev = rows // BLK
    npick = picks.shape[1]
    scale = HEAD_SIZE ** (-0.5)
    q_blocks = query_rows.reshape(per_dev, BLK, kvh, group_size, HEAD_SIZE)
    score = (
        jnp.einsum("bqkgd,blkd->bkgql", q_blocks, kk, preferred_element_type=jnp.float32) * scale
    )
    sent = sentences.reshape(per_dev, BLK)
    idx = jnp.arange(BLK, dtype=jnp.int32)
    band = (idx[None, :, None] >= idx[None, None, :]) & (sent[:, :, None] == sent[:, None, :])
    valid = jnp.repeat(anchor_blocks[picks] < blocks[:, None], BLK, axis=1)
    far_mask = jnp.broadcast_to(valid[:, None, :], (per_dev, BLK, npick * BLK))
    mask = jnp.concatenate([band, far_mask], axis=2)[:, None, None]
    score = jnp.where(mask, score, jnp.float32(-1e30))
    top = jnp.max(score, axis=-1, keepdims=True)
    expo = jnp.exp(score - top)
    return expo / jnp.sum(expo, axis=-1, keepdims=True)


def backward(query_rows, kk, vv, probs, cot):
    rows, width = query_rows.shape
    kvh = kk.shape[2]
    feat = 2 * kvh * HEAD_SIZE
    group_size = width // (kvh * HEAD_SIZE)
    per_dev = rows // BLK
    scale = HEAD_SIZE ** (-0.5)
    q_blocks = query_rows.reshape(per_dev, BLK, kvh, group_size, HEAD_SIZE)
    pb = probs.astype(jnp.bfloat16)
    outp = jnp.einsum("bkgql,blkd->bqkgd", pb, vv, preferred_element_type=jnp.float32)
    c_blocks = cot.reshape(per_dev, BLK, kvh, group_size, HEAD_SIZE)
    delta = jnp.sum(c_blocks.astype(jnp.float32) * outp, axis=-1).transpose(0, 2, 3, 1)[..., None]
    dprob = jnp.einsum("bqkgd,blkd->bkgql", c_blocks, vv, preferred_element_type=jnp.float32)
    dscore = (probs * (dprob - delta)).astype(jnp.bfloat16)
    dq = jnp.einsum("bkgql,blkd->bqkgd", dscore, kk, preferred_element_type=jnp.float32) * scale
    dk = (
        jnp.einsum("bkgql,bqkgd->blkd", dscore, q_blocks, preferred_element_type=jnp.float32)
        * scale
    )
    dv = jnp.einsum("bkgql,bqkgd->blkd", pb, c_blocks, preferred_element_type=jnp.float32)
    dkv = jnp.stack([dk, dv], axis=3)
    band_grad = dkv[:, :BLK].reshape(rows, feat)
    far_grad = dkv[:, BLK:].reshape(-1, BLK, feat)
    return (dq.reshape(rows, width), band_grad, far_grad)


def spread_anchors(mine, rows_per_slot):
    ny = lax.axis_size("cy")
    nx = lax.axis_size("cx")
    blk, feat = mine.shape
    part = mine.reshape(ny, blk // ny, feat)
    got = lax.all_to_all(part, "cy", 0, 0, tiled=True)
    row = jnp.sum(got.astype(jnp.float32), axis=0).astype(mine.dtype)
    got = lax.all_to_all(jnp.broadcast_to(row[None], (nx,) + row.shape), "cx", 0, 0, tiled=True)
    nslot = nx // rows_per_slot
    slots = jnp.sum(
        got.reshape(nslot, rows_per_slot, *row.shape).astype(jnp.float32), axis=1
    ).astype(mine.dtype)
    got = lax.all_to_all(jnp.broadcast_to(slots[None], (ny,) + slots.shape), "cy", 0, 0, tiled=True)
    return got.transpose(1, 0, 2, 3).reshape(nslot, blk, feat)


def gather_grads(far, picks, nslot, rows_per_slot):
    ny = lax.axis_size("cy")
    npick, blk, feat = far.shape
    rows = blk // ny
    data = far.astype(jnp.bfloat16).reshape(npick, ny, rows, feat)
    tag = jnp.broadcast_to(picks.astype(jnp.bfloat16)[:, None, None, None], (npick, ny, rows, 128))
    load = jnp.concatenate([data, tag], axis=3).transpose(1, 0, 2, 3)
    got = lax.all_to_all(load, "cy", 0, 0, tiled=True)
    vals = got[..., :feat].astype(jnp.float32)
    ids = got[:, :, 0, feat].astype(jnp.float32)
    slot_ids = jnp.arange(nslot, dtype=jnp.float32)
    rowsum = jnp.sum(
        jnp.where(ids[None, :, :, None, None] == slot_ids[:, None, None, None, None], vals[None], 0.0),
        axis=(1, 2),
    )
    part = jnp.repeat(rowsum.astype(jnp.bfloat16), rows_per_slot, axis=0)
    got = lax.all_to_all(part, "cx", 0, 0, tiled=True)
    total = jnp.sum(got.astype(jnp.float32), axis=0).astype(jnp.bfloat16)
    got = lax.all_to_all(jnp.broadcast_to(total[None], (ny,) + total.shape), "cy", 0, 0, tiled=True)
    return got.reshape(blk, feat).astype(jnp.float32)


def body(layer_in, kv_in, out_grad, sentences, anchor_blocks, anchor_pick):
    query_rows = layer_in[0]
    keyvals = kv_in[0]
    rows, width = query_rows.shape
    feat = keyvals.shape[1]
    per_dev = rows // BLK
    nanch = anchor_blocks.shape[0]
    rows_per_slot = lax.axis_size("cx") // nanch
    ctx = lax.axis_index("cx") * lax.axis_size("cy") + lax.axis_index("cy")
    rank = lax.axis_index("cx") // rows_per_slot
    section_one = lax.axis_index("section") == 1
    blocks = ctx * per_dev + jnp.arange(per_dev, dtype=jnp.int32)
    kv_blocks = keyvals.reshape(per_dev, BLK, feat)
    hit = anchor_blocks[None, :] == blocks[:, None]
    holder = jnp.any(hit, axis=1)[:, None, None]
    mine = jnp.where(holder, kv_blocks, jnp.zeros_like(kv_blocks)).sum(axis=0, dtype=jnp.float32)
    mine = mine.astype(jnp.bfloat16)
    anchor_kv = spread_anchors(mine, rows_per_slot)
    npick = anchor_pick.shape[1]
    kk, vv = gather_keys(keyvals, anchor_kv, anchor_pick)

    def probs_of():
        return forward(query_rows, kk, sentences, anchor_pick, anchor_blocks, blocks)

    def relayed(probs, cot):
        dq, band, far = backward(query_rows, kk, vv, probs, cot)
        return dq.astype(jnp.bfloat16), band, far

    def second_layer(cot):
        probs = probs_of()
        return (probs,) + relayed(probs, cot)

    def first_layer_probs(cot):
        return (
            probs_of(),
            cot,
            jnp.zeros((rows, feat), jnp.float32),
            jnp.zeros((per_dev * npick, BLK, feat), jnp.float32),
        )

    probs, sent_back, band_first, far_first = lax.cond(
        section_one, second_layer, first_layer_probs, out_grad
    )
    arrived = from_behind(sent_back, "section", -1)
    dq_out, band_grad, far = lax.cond(
        section_one,
        lambda cot: (sent_back, band_first, far_first),
        lambda cot: relayed(probs, cot),
        arrived,
    )
    total = gather_grads(far, anchor_pick.reshape(-1), nanch, rows_per_slot)
    owner = (anchor_blocks[rank] == blocks).astype(jnp.float32)
    owned = owner[:, None, None] * total[None]
    kv_grad = (band_grad + owned.reshape(band_grad.shape)).astype(jnp.bfloat16)
    input_grad = dq_out
    return (input_grad[None], kv_grad[None])


def solution(mesh):
    ny = 8
    devs = mesh.devices
    grid = Mesh(
        devs.reshape(devs.shape[0], devs.shape[1] // ny, ny, devs.shape[2]),
        ("section", "cx", "cy", "head"),
    )
    ctx = ("cx", "cy")
    placed = (
        P("section", ctx, "head"),
        P("section", ctx, "head"),
        P(ctx, "head"),
        P(ctx),
        P(),
        P(ctx, None),
    )
    return jax.shard_map(
        body,
        mesh=grid,
        in_specs=placed,
        out_specs=(P("section", ctx, "head"), P("section", ctx, "head")),
        check_vma=False,
    )
```
